256 devices in a mesh: dom: 32 (over x_lo, z, core), band: 8 (over x_hi, y).
Axes of the slice: x: 4 (x_hi: 2, x_lo: 2; x = x_hi * 2 + x_lo), y: 4, z: 8, core: 2. Of those that a mesh axis runs over, the one named last changes fastest.
Arguments:
- ensemble: float32 [32, 3, 128, 4096], P('dom', None, 'band'), may hold values from -6 to 6
- ancestors: int32 [32], P('dom'), may hold values from 0 to 31
- sea_depth: float32 [128, 4096], P('band'), may hold values from 1 to 2
- obs_rows: int32 [16384], P('band'), may hold values from 0 to 127, as said below
- obs_cols: int32 [16384], P('band'), may hold values from 0 to 4095
- obs_values: float32 [16384], P('band'), may hold values from -6 to 6
Outputs:
- forecast: float32 [32, 3, 128, 4096], P('dom', None, 'band')
The draws below stay inside these ranges and needn't reach their ends.
Inputs may be any that keep to these rules, and one draw needn't show every extreme that they name: `obs_rows`: observations b * 2048 to (b + 1) * 2048 - 1 lie in rows b * 16 to (b + 1) * 16 - 1; no two observations share a cell.
All inputs are finite; a program needn't handle non-finite values.
Results may differ from the reference program's by a relative error of at most 0.00016.
Values sent between devices are 32-bit elements; how exact they have to be, the bound alone decides.
No kernel may reach another device: no remote copies, remote signals or barrier semaphores. Data moves between devices by JAX's collectives and lax.ppermute only.
A program may use at most 64 MiB of HBM per device.

```python
import math
import jax
import jax.numpy as jnp
import numpy as np
from jax import lax

ROWS_DEV = 16
NCOL = 4096
OBS_BAND = 2048
STEPS = 4
BW = 8
PARTICLES = 32
NROWS = 128
NOBS = 16384


def obs_cells(key):
    band_count = NROWS // ROWS_DEV
    band_keys = jax.random.split(jax.random.fold_in(key, 7), band_count)

    def one_band(band_key):
        return jax.random.permutation(band_key, ROWS_DEV * NCOL)[:OBS_BAND]
    cells = jax.vmap(one_band)(band_keys)
    offsets = (jnp.arange(band_count) * ROWS_DEV)[:, None]
    row_part = (cells // NCOL + offsets).reshape(-1).astype(jnp.int32)
    col_part = (cells % NCOL).reshape(-1).astype(jnp.int32)
    return (row_part, col_part)


def draw_obs_rows(key, part):
    return obs_cells(key)[0]


def draw_obs_cols(key, part):
    return obs_cells(key)[1]


def touch_ends(values, own_key, least, largest):
    longest = values.shape.index(max(values.shape))
    spots = []
    for shift in (0, 1):
        where = [jax.random.randint(jax.random.fold_in(own_key, axis), (), 0, length) for axis, length in enumerate(values.shape)]
        where[longest] = (where[longest] + shift) % values.shape[longest]
        spots.append(tuple(where))
    return values.at[spots[0]].set(least).at[spots[1]].set(largest)


def shard_levels(stream_key, extent, cuts, low, top_value):
    def one(position, shards_of):
        steps = jax.random.uniform(jax.random.fold_in(jax.random.fold_in(stream_key, 6), position), (shards_of,), jnp.float32, low / len(cuts), top_value / len(cuts))
        return jnp.repeat(jnp.exp(steps), extent[position] // shards_of).reshape((-1,) + (1,) * (len(extent) - position - 1))

    level = one(*cuts[0])
    for cut in cuts[1:]:
        level = level * one(*cut)
    return level


def rank_table(count, skew):
    weights = [(1 << 20) // math.isqrt(grade ** skew) + 1 for grade in range(1, count + 1)]
    width = 1 + sum(weights) // (1 << 30)
    return np.cumsum(np.array([max(1, weight // width) for weight in weights]))


def skewed_ids(stream_key, shape, count, slope):
    listing = rank_table(count, slope)
    ticket = jax.random.randint(jax.random.fold_in(stream_key, 1), shape, 0, int(listing[count - 1]))
    rank = jnp.searchsorted(jnp.asarray(listing, jnp.int32), ticket, side="right")
    return jax.random.permutation(jax.random.fold_in(stream_key, 2), count)[rank].astype(jnp.int32)


def normal_values(key, dims, width, reach, cuts=(), kind=jnp.bfloat16):
    level = shard_levels(key, dims, cuts, -0.22, 0.18) if cuts else 1.0
    entries = jax.random.normal(key, dims, jnp.float32) * width * level
    return jnp.minimum(jnp.maximum(entries, -reach), reach).astype(kind)


def setup_inputs(seed: int = 0) -> dict:
    key_of = jax.random.split(jax.random.key(seed), 7)
    return {
        "ensemble": normal_values(key_of[0], (PARTICLES, 3, NROWS, NCOL), 1.0, 6.0, ((0, 32), (2, 8)), jnp.float32),
        "ancestors": touch_ends(skewed_ids(key_of[1], (PARTICLES,), PARTICLES, 2), jax.random.fold_in(key_of[1], 3), 0, PARTICLES - 1).astype(jnp.int32),
        "sea_depth": jnp.clip(jnp.exp(math.log(2.0) - 0.6931472 * jax.random.uniform(key_of[2], (NROWS, NCOL), jnp.float32) ** shard_levels(key_of[2], (NROWS, NCOL), ((0, 8),), -0.2, 0.2)), 1.0, 2.0),
        "obs_rows": draw_obs_rows(jax.random.fold_in(key_of[6], 71), 0),
        "obs_cols": draw_obs_cols(jax.random.fold_in(key_of[6], 71), 0),
        "obs_values": normal_values(key_of[5], (NOBS,), 1.0, 6.0, ((0, 8),), jnp.float32),
    }


TIME_STEP = 0.8
NUDGE_GAIN = 0.5
LENGTH_SCALE = 3.0


def kernel_weight(offset):
    return jnp.exp(jnp.float32(-abs(offset) / LENGTH_SCALE))


def band_smooth(field, axis_no):
    count = field.shape[axis_no]
    widths = [(0, 0), (0, 0)]
    widths[axis_no] = (BW, BW)
    padded = jnp.pad(field, widths)
    total = jnp.zeros_like(field)
    for offset in range(-BW, BW + 1):
        piece = lax.slice_in_dim(padded, BW + offset, BW + offset + count, axis=axis_no)
        total = total + kernel_weight(offset) * piece
    return total


def advance(height, east_vel, north_vel, sea_depth, coriolis):
    flux_east = sea_depth * east_vel
    flux_north = jnp.pad(sea_depth * north_vel, ((1, 1), (0, 0)))
    east_diff = 0.5 * (jnp.roll(flux_east, -1, -1) - jnp.roll(flux_east, 1, -1))
    north_diff = 0.5 * (flux_north[2:] - flux_north[:-2])
    new_height = height - TIME_STEP * (east_diff + north_diff)
    padded = jnp.pad(new_height, ((1, 1), (0, 0)))
    slope_east = 0.5 * (jnp.roll(new_height, -1, -1) - jnp.roll(new_height, 1, -1))
    slope_north = 0.5 * (padded[2:] - padded[:-2])
    new_east = east_vel + TIME_STEP * (coriolis * north_vel - slope_east)
    new_north = north_vel + TIME_STEP * (-coriolis * east_vel - slope_north)
    return new_height, new_east, new_north


def reference(ensemble, ancestors, sea_depth, obs_rows, obs_cols, obs_values):
    children = ensemble[ancestors]
    row_index = jnp.arange(NROWS)
    coriolis = (0.1 + 0.4 * ((row_index.astype(jnp.float32) + 0.5) / NROWS))[:, None]

    def evolve_one(particle):
        height, east_vel, north_vel = particle[0], particle[1], particle[2]
        innovation = obs_values - height[obs_rows, obs_cols]
        scattered = jnp.zeros((NROWS, NCOL), jnp.float32).at[obs_rows, obs_cols].add(innovation)
        spread = band_smooth(scattered, 1)
        increment = band_smooth(spread, 0)
        height = height + NUDGE_GAIN * increment
        for section_no in range(STEPS):
            height, east_vel, north_vel = advance(height, east_vel, north_vel, sea_depth, coriolis)
        return jnp.stack([height, east_vel, north_vel])

    return lax.map(evolve_one, children)
```

```python
import numpy as np
import jax
import jax.numpy as jnp
from jax import lax
from jax.sharding import PartitionSpec as P

STEPS = 4
BW = 8


TIME_STEP = 0.8
NUDGE_GAIN = 0.5
LENGTH_SCALE = 3.0


def weights():
    return [np.float32(np.exp(np.float32(-abs(o) / LENGTH_SCALE))) for o in range(-BW, BW + 1)]


def smooth(field, axis_no):
    count = field.shape[axis_no]
    widths = [(0, 0)] * field.ndim
    widths[axis_no] = (BW, BW)
    padded = jnp.pad(field, widths)
    total = jnp.zeros_like(field)
    for offset, weight in zip(range(-BW, BW + 1), weights()):
        piece = lax.slice_in_dim(padded, BW + offset, BW + offset + count, axis=axis_no)
        total = total + weight * piece
    return total


def shift_rows(q, d):
    if d > 0:
        return jnp.concatenate([q[d:], jnp.zeros_like(q[:d])], axis=0)
    return jnp.concatenate([jnp.zeros_like(q[:(-d)]), q[:d]], axis=0)


def advance(height, east_vel, north_vel, depth, coriolis, inside):
    flux_east = depth * east_vel
    flux_north = depth * north_vel
    east_diff = 0.5 * (jnp.roll(flux_east, -1, -1) - jnp.roll(flux_east, 1, -1))
    north_diff = 0.5 * (shift_rows(flux_north, 1) - shift_rows(flux_north, -1))
    new_height = jnp.where(inside, height - TIME_STEP * (east_diff + north_diff), jnp.float32(0.0))
    slope_east = 0.5 * (jnp.roll(new_height, -1, -1) - jnp.roll(new_height, 1, -1))
    slope_north = 0.5 * (shift_rows(new_height, 1) - shift_rows(new_height, -1))
    new_east = east_vel + TIME_STEP * (coriolis * north_vel - slope_east)
    new_north = north_vel + TIME_STEP * (-coriolis * east_vel - slope_north)
    return new_height, new_east, new_north


def on_device(ensemble, ancestors, sea_depth, obs_rows, obs_cols, obs_values):
    _, fields, rows, columns = ensemble.shape
    parts = lax.axis_size("dom")
    bands = lax.axis_size("band")
    band = lax.axis_index("band")
    down = [(i, i + 1) for i in range(bands - 1)]
    up = [(i + 1, i) for i in range(bands - 1)]
    margin = 2 * STEPS

    block = ensemble.reshape(fields * rows, parts, columns // parts).transpose(1, 0, 2)
    lineage = lax.all_gather(ancestors, "dom", axis=0, tiled=True)
    crossed = lax.all_to_all(block, "dom", 0, 0, tiled=True)
    chosen = jnp.take(crossed, lineage, axis=0)
    back = lax.all_to_all(chosen, "dom", 0, 0, tiled=True)
    state = back.transpose(1, 0, 2).reshape(fields, rows, columns)

    band_start = band * rows
    position = (obs_rows - band_start) * columns + obs_cols
    observed = jnp.zeros((rows * columns,), jnp.bool_).at[position].set(True).reshape(rows, columns)
    values = jnp.zeros((rows * columns,), jnp.float32).at[position].set(obs_values).reshape(rows, columns)

    depth_ext = jnp.concatenate(
        [
            lax.ppermute(sea_depth[rows - margin:], "band", down),
            sea_depth,
            lax.ppermute(sea_depth[:margin], "band", up),
        ],
        axis=0,
    )

    height, east_vel, north_vel = state[0], state[1], state[2]
    scattered = jnp.where(observed, values - height, jnp.float32(0.0))
    spread = smooth(scattered, 1)

    to_below = jnp.concatenate(
        [spread, height[rows - margin:], east_vel[rows - margin:], north_vel[rows - margin:]], axis=0
    )
    to_above = jnp.concatenate(
        [spread, height[:margin], east_vel[:margin], north_vel[:margin]], axis=0
    )
    from_above = lax.ppermute(to_below, "band", down)
    from_below = lax.ppermute(to_above, "band", up)

    spread_ext = jnp.concatenate([from_above[:rows], spread, from_below[:rows]], axis=0)
    increment = smooth(spread_ext, 0)[rows - margin: 2 * rows + margin]

    def ext(i, own):
        lo = rows + i * margin
        return jnp.concatenate([from_above[lo:lo + margin], own, from_below[lo:lo + margin]], axis=0)

    height = ext(0, height) + NUDGE_GAIN * increment
    east_vel = ext(1, east_vel)
    north_vel = ext(2, north_vel)

    total_rows = rows * bands
    global_rows = band_start - margin + jnp.arange(rows + 2 * margin)
    inside = ((global_rows >= 0) & (global_rows < total_rows))[:, None]
    coriolis = (0.1 + 0.4 * ((global_rows.astype(jnp.float32) + 0.5) / total_rows))[:, None]
    for _ in range(STEPS):
        height, east_vel, north_vel = advance(height, east_vel, north_vel, depth_ext, coriolis, inside)
    out = jnp.stack([height, east_vel, north_vel], axis=0)[:, margin:margin + rows]
    return out[None]


def solution(mesh):
    placed = (
        P("dom", None, "band", None),
        P("dom"),
        P("band", None),
        P("band"),
        P("band"),
        P("band"),
    )
    return jax.shard_map(
        on_device,
        mesh=mesh,
        in_specs=placed,
        out_specs=P("dom", None, "band", None),
        check_vma=False,
    )
```

```python
import numpy as np
import jax
import jax.numpy as jnp
from jax import lax
from jax.sharding import PartitionSpec as P

STEPS = 4
BW = 8


TIME_STEP = 0.8
NUDGE_GAIN = 0.5
LENGTH_SCALE = 3.0


def weights():
    return [np.float32(np.exp(np.float32(-abs(o) / LENGTH_SCALE))) for o in range(-BW, BW + 1)]


def smooth(field, axis_no):
    count = field.shape[axis_no]
    widths = [(0, 0)] * field.ndim
    widths[axis_no] = (BW, BW)
    padded = jnp.pad(field, widths)
    total = jnp.zeros_like(field)
    for offset, weight in zip(range(-BW, BW + 1), weights()):
        piece = lax.slice_in_dim(padded, BW + offset, BW + offset + count, axis=axis_no)
        total = total + weight * piece
    return total


def shift_rows(q, d):
    if d > 0:
        return jnp.concatenate([q[d:], jnp.zeros_like(q[:d])], axis=0)
    return jnp.concatenate([jnp.zeros_like(q[:(-d)]), q[:d]], axis=0)


def advance(height, east_vel, north_vel, depth, coriolis, inside):
    flux_east = depth * east_vel
    flux_north = depth * north_vel
    east_diff = 0.5 * (jnp.roll(flux_east, -1, -1) - jnp.roll(flux_east, 1, -1))
    north_diff = 0.5 * (shift_rows(flux_north, 1) - shift_rows(flux_north, -1))
    new_height = jnp.where(inside, height - TIME_STEP * (east_diff + north_diff), jnp.float32(0.0))
    slope_east = 0.5 * (jnp.roll(new_height, -1, -1) - jnp.roll(new_height, 1, -1))
    slope_north = 0.5 * (shift_rows(new_height, 1) - shift_rows(new_height, -1))
    new_east = east_vel + TIME_STEP * (coriolis * north_vel - slope_east)
    new_north = north_vel + TIME_STEP * (-coriolis * east_vel - slope_north)
    return new_height, new_east, new_north


def on_device(ensemble, ancestors, sea_depth, obs_rows, obs_cols, obs_values):
    _, fields, rows, columns = ensemble.shape
    parts = lax.axis_size("dom")
    bands = lax.axis_size("band")
    band = lax.axis_index("band")
    down = [(i, i + 1) for i in range(bands - 1)]
    up = [(i + 1, i) for i in range(bands - 1)]
    margin = 2 * STEPS

    block = ensemble.reshape(fields * rows, parts, columns // parts).transpose(1, 0, 2)
    tag = jnp.broadcast_to(ancestors.astype(jnp.float32)[:, None, None], (parts, 8, columns // parts))
    crossed = lax.all_to_all(jnp.concatenate([block, tag], axis=1), "dom", 0, 0, tiled=True)
    lineage = crossed[:, fields * rows, 0].astype(jnp.int32)
    chosen = jnp.take(crossed[:, :fields * rows], lineage, axis=0)
    back = lax.all_to_all(chosen, "dom", 0, 0, tiled=True)
    state = back.transpose(1, 0, 2).reshape(fields, rows, columns)

    band_start = band * rows
    position = (obs_rows - band_start) * columns + obs_cols
    observed = jnp.zeros((rows * columns,), jnp.bool_).at[position].set(True).reshape(rows, columns)
    values = jnp.zeros((rows * columns,), jnp.float32).at[position].set(obs_values).reshape(rows, columns)

    depth_ext = jnp.concatenate(
        [
            lax.ppermute(sea_depth[rows - margin:], "band", down),
            sea_depth,
            lax.ppermute(sea_depth[:margin], "band", up),
        ],
        axis=0,
    )

    height, east_vel, north_vel = state[0], state[1], state[2]
    scattered = jnp.where(observed, values - height, jnp.float32(0.0))
    spread = smooth(scattered, 1)

    to_below = jnp.concatenate(
        [spread, height[rows - margin:], east_vel[rows - margin:], north_vel[rows - margin:]], axis=0
    )
    to_above = jnp.concatenate(
        [spread, height[:margin], east_vel[:margin], north_vel[:margin]], axis=0
    )
    from_above = lax.ppermute(to_below, "band", down)
    from_below = lax.ppermute(to_above, "band", up)

    spread_ext = jnp.concatenate([from_above[:rows], spread, from_below[:rows]], axis=0)
    increment = smooth(spread_ext, 0)[rows - margin: 2 * rows + margin]

    def ext(i, own):
        lo = rows + i * margin
        return jnp.concatenate([from_above[lo:lo + margin], own, from_below[lo:lo + margin]], axis=0)

    height = ext(0, height) + NUDGE_GAIN * increment
    east_vel = ext(1, east_vel)
    north_vel = ext(2, north_vel)

    total_rows = rows * bands
    global_rows = band_start - margin + jnp.arange(rows + 2 * margin)
    inside = ((global_rows >= 0) & (global_rows < total_rows))[:, None]
    coriolis = (0.1 + 0.4 * ((global_rows.astype(jnp.float32) + 0.5) / total_rows))[:, None]
    for _ in range(STEPS):
        height, east_vel, north_vel = advance(height, east_vel, north_vel, depth_ext, coriolis, inside)
    out = jnp.stack([height, east_vel, north_vel], axis=0)[:, margin:margin + rows]
    return out[None]


def solution(mesh):
    placed = (
        P("dom", None, "band", None),
        P("dom"),
        P("band", None),
        P("band"),
        P("band"),
        P("band"),
    )
    return jax.shard_map(
        on_device,
        mesh=mesh,
        in_specs=placed,
        out_specs=P("dom", None, "band", None),
        check_vma=False,
    )
```

```python
import numpy as np
import jax
import jax.numpy as jnp
from jax import lax
from jax.sharding import PartitionSpec as P
from jax.experimental import pallas as pl
from jax.experimental.pallas import tpu as pltpu

STEPS = 4
BW = 8


TIME_STEP = 0.8
NUDGE_GAIN = 0.5
LENGTH_SCALE = 3.0
INTERPRET = False


def weights():
    return [np.float32(np.exp(np.float32(-abs(o) / LENGTH_SCALE))) for o in range(-BW, BW + 1)]


def smooth(field, axis_no):
    count = field.shape[axis_no]
    widths = [(0, 0)] * field.ndim
    widths[axis_no] = (BW, BW)
    padded = jnp.pad(field, widths)
    total = jnp.zeros_like(field)
    for offset, weight in zip(range(-BW, BW + 1), weights()):
        piece = lax.slice_in_dim(padded, BW + offset, BW + offset + count, axis=axis_no)
        total = total + weight * piece
    return total


def forecast_kernel(fa_ref, fb_ref, h_ref, u_ref, v_ref, sp_ref, d_ref, cor_ref, ins_ref,
                    o_ref, sext_ref, pad_ref, hx_ref, ux_ref, vx_ref):
    rows = h_ref.shape[0]
    margin = 2 * STEPS
    ext = rows + 2 * margin
    columns = h_ref.shape[1]
    sext_ref[0:rows] = fa_ref[0:rows]
    sext_ref[rows:2 * rows] = sp_ref[...]
    sext_ref[2 * rows:3 * rows] = fb_ref[0:rows]
    increment = jnp.zeros((ext, columns), jnp.float32)
    for offset, weight in zip(range(-BW, BW + 1), weights()):
        lo = rows - margin + offset
        increment = increment + weight * sext_ref[lo:lo + ext]
    for i, (x_ref, own_ref) in enumerate(((hx_ref, h_ref), (ux_ref, u_ref), (vx_ref, v_ref))):
        lo = rows + i * margin
        x_ref[0:margin] = fa_ref[lo:lo + margin]
        x_ref[margin:margin + rows] = own_ref[...]
        x_ref[margin + rows:ext] = fb_ref[lo:lo + margin]
    height = hx_ref[...] + NUDGE_GAIN * increment
    east_vel = ux_ref[...]
    north_vel = vx_ref[...]
    depth = d_ref[...]
    coriolis = cor_ref[...]
    inside = ins_ref[...] > 0.5
    pad_ref[0:8] = jnp.zeros((8, columns), jnp.float32)
    pad_ref[8 + ext:16 + ext] = jnp.zeros((8, columns), jnp.float32)

    def north(q):
        pad_ref[8:8 + ext] = q
        return 0.5 * (pad_ref[9:9 + ext] - pad_ref[7:7 + ext])

    def east(q):
        return 0.5 * (pltpu.roll(q, columns - 1, 1) - pltpu.roll(q, 1, 1))

    for _ in range(STEPS):
        flux_east = depth * east_vel
        flux_north = depth * north_vel
        east_diff = east(flux_east)
        north_diff = north(flux_north)
        height = jnp.where(inside, height - TIME_STEP * (east_diff + north_diff), jnp.float32(0.0))
        slope_east = east(height)
        slope_north = north(height)
        new_east = east_vel + TIME_STEP * (coriolis * north_vel - slope_east)
        new_north = north_vel + TIME_STEP * (-coriolis * east_vel - slope_north)
        east_vel, north_vel = new_east, new_north
    o_ref[0] = height[margin:margin + rows]
    o_ref[1] = east_vel[margin:margin + rows]
    o_ref[2] = north_vel[margin:margin + rows]


def on_device(ensemble, ancestors, sea_depth, obs_rows, obs_cols, obs_values):
    _, fields, rows, columns = ensemble.shape
    parts = lax.axis_size("dom")
    bands = lax.axis_size("band")
    band = lax.axis_index("band")
    down = [(i, i + 1) for i in range(bands - 1)]
    up = [(i + 1, i) for i in range(bands - 1)]
    margin = 2 * STEPS

    block = ensemble.reshape(fields * rows, parts, columns // parts).transpose(1, 0, 2)
    tag = jnp.broadcast_to(ancestors.astype(jnp.float32)[:, None, None], (parts, 8, columns // parts))
    crossed = lax.all_to_all(jnp.concatenate([block, tag], axis=1), "dom", 0, 0, tiled=True)
    lineage = crossed[:, fields * rows, 0].astype(jnp.int32)
    chosen = jnp.take(crossed[:, :fields * rows], lineage, axis=0)
    back = lax.all_to_all(chosen, "dom", 0, 0, tiled=True)
    state = back.transpose(1, 0, 2).reshape(fields, rows, columns)

    band_start = band * rows
    position = (obs_rows - band_start) * columns + obs_cols
    observed = jnp.zeros((rows * columns,), jnp.bool_).at[position].set(True).reshape(rows, columns)
    values = jnp.zeros((rows * columns,), jnp.float32).at[position].set(obs_values).reshape(rows, columns)

    depth_ext = jnp.concatenate(
        [
            lax.ppermute(sea_depth[rows - margin:], "band", down),
            sea_depth,
            lax.ppermute(sea_depth[:margin], "band", up),
        ],
        axis=0,
    )

    height, east_vel, north_vel = state[0], state[1], state[2]
    scattered = jnp.where(observed, values - height, jnp.float32(0.0))
    spread = smooth(scattered, 1)

    to_below = jnp.concatenate(
        [spread, height[rows - margin:], east_vel[rows - margin:], north_vel[rows - margin:]], axis=0
    )
    to_above = jnp.concatenate(
        [spread, height[:margin], east_vel[:margin], north_vel[:margin]], axis=0
    )
    from_above = lax.ppermute(to_below, "band", down)
    from_below = lax.ppermute(to_above, "band", up)

    total_rows = rows * bands
    ext_rows = rows + 2 * margin
    global_rows = band_start - margin + jnp.arange(ext_rows)
    inside = ((global_rows >= 0) & (global_rows < total_rows)).astype(jnp.float32)[:, None]
    coriolis = (0.1 + 0.4 * ((global_rows.astype(jnp.float32) + 0.5) / total_rows))[:, None]
    wide = (ext_rows, columns)
    out = pl.pallas_call(
        forecast_kernel,
        interpret=INTERPRET,
        out_shape=jax.ShapeDtypeStruct((fields, rows, columns), jnp.float32),
        scratch_shapes=[
            pltpu.VMEM((3 * rows, columns), jnp.float32),
            pltpu.VMEM((ext_rows + 16, columns), jnp.float32),
            pltpu.VMEM(wide, jnp.float32),
            pltpu.VMEM(wide, jnp.float32),
            pltpu.VMEM(wide, jnp.float32),
        ],
    )(
        from_above, from_below, height, east_vel, north_vel, spread, depth_ext,
        jnp.broadcast_to(coriolis, wide), jnp.broadcast_to(inside, wide),
    )
    return out[None]


def solution(mesh):
    placed = (
        P("dom", None, "band", None),
        P("dom"),
        P("band", None),
        P("band"),
        P("band"),
        P("band"),
    )
    return jax.shard_map(
        on_device,
        mesh=mesh,
        in_specs=placed,
        out_specs=P("dom", None, "band", None),
        check_vma=False,
    )
```

```python
import numpy as np
import jax
import jax.numpy as jnp
from jax import lax
from jax.sharding import PartitionSpec as P
from jax.experimental import pallas as pl
from jax.experimental.pallas import tpu as pltpu

STEPS = 4
BW = 8


TIME_STEP = 0.8
NUDGE_GAIN = 0.5
LENGTH_SCALE = 3.0
INTERPRET = False


def weights():
    return [np.float32(np.exp(np.float32(-abs(o) / LENGTH_SCALE))) for o in range(-BW, BW + 1)]


def smooth(field, axis_no):
    count = field.shape[axis_no]
    widths = [(0, 0)] * field.ndim
    widths[axis_no] = (BW, BW)
    padded = jnp.pad(field, widths)
    total = jnp.zeros_like(field)
    for offset, weight in zip(range(-BW, BW + 1), weights()):
        piece = lax.slice_in_dim(padded, BW + offset, BW + offset + count, axis=axis_no)
        total = total + weight * piece
    return total


def forecast_kernel(fa_ref, fb_ref, h_ref, u_ref, v_ref, sp_ref, d_ref, cor_ref, ins_ref,
                    o_ref, sext_ref, pad_ref, hx_ref, ux_ref, vx_ref):
    rows = h_ref.shape[0]
    margin = 2 * STEPS
    ext = rows + 2 * margin
    columns = h_ref.shape[1]
    sext_ref[0:rows] = fa_ref[0:rows]
    sext_ref[rows:2 * rows] = sp_ref[...]
    sext_ref[2 * rows:3 * rows] = fb_ref[0:rows]
    increment = jnp.zeros((ext, columns), jnp.float32)
    for offset, weight in zip(range(-BW, BW + 1), weights()):
        lo = rows - margin + offset
        increment = increment + weight * sext_ref[lo:lo + ext]
    for i, (x_ref, own_ref) in enumerate(((hx_ref, h_ref), (ux_ref, u_ref), (vx_ref, v_ref))):
        lo = rows + i * margin
        x_ref[0:margin] = fa_ref[lo:lo + margin]
        x_ref[margin:margin + rows] = own_ref[...]
        x_ref[margin + rows:ext] = fb_ref[lo:lo + margin]
    height = hx_ref[...] + NUDGE_GAIN * increment
    east_vel = ux_ref[...]
    north_vel = vx_ref[...]
    depth = d_ref[...]
    coriolis = jnp.broadcast_to(cor_ref[:, 0:1], (ext, columns))
    inside = jnp.broadcast_to(ins_ref[:, 0:1], (ext, columns)) > 0.5
    pad_ref[0:8] = jnp.zeros((8, columns), jnp.float32)
    pad_ref[8 + ext:16 + ext] = jnp.zeros((8, columns), jnp.float32)

    def north(q):
        pad_ref[8:8 + ext] = q
        return 0.5 * (pad_ref[9:9 + ext] - pad_ref[7:7 + ext])

    def east(q):
        return 0.5 * (pltpu.roll(q, columns - 1, 1) - pltpu.roll(q, 1, 1))

    for _ in range(STEPS):
        flux_east = depth * east_vel
        flux_north = depth * north_vel
        east_diff = east(flux_east)
        north_diff = north(flux_north)
        height = jnp.where(inside, height - TIME_STEP * (east_diff + north_diff), jnp.float32(0.0))
        slope_east = east(height)
        slope_north = north(height)
        new_east = east_vel + TIME_STEP * (coriolis * north_vel - slope_east)
        new_north = north_vel + TIME_STEP * (-coriolis * east_vel - slope_north)
        east_vel, north_vel = new_east, new_north
    o_ref[0] = height[margin:margin + rows]
    o_ref[1] = east_vel[margin:margin + rows]
    o_ref[2] = north_vel[margin:margin + rows]


def on_device(ensemble, ancestors, sea_depth, obs_rows, obs_cols, obs_values):
    _, fields, rows, columns = ensemble.shape
    parts = lax.axis_size("dom")
    bands = lax.axis_size("band")
    band = lax.axis_index("band")
    down = [(i, i + 1) for i in range(bands - 1)]
    up = [(i + 1, i) for i in range(bands - 1)]
    margin = 2 * STEPS

    block = ensemble.reshape(fields * rows, parts, columns // parts).transpose(1, 0, 2)
    tag = jnp.broadcast_to(ancestors.astype(jnp.float32)[:, None, None], (parts, 8, columns // parts))
    crossed = lax.all_to_all(jnp.concatenate([block, tag], axis=1), "dom", 0, 0, tiled=True)
    lineage = crossed[:, fields * rows, 0].astype(jnp.int32)
    chosen = jnp.take(crossed[:, :fields * rows], lineage, axis=0)
    back = lax.all_to_all(chosen, "dom", 0, 0, tiled=True)
    state = back.transpose(1, 0, 2).reshape(fields, rows, columns)

    band_start = band * rows
    position = (obs_rows - band_start) * columns + obs_cols
    values = jnp.full((rows * columns,), jnp.nan, jnp.float32).at[position].set(obs_values)
    values = values.reshape(rows, columns)

    depth_ext = jnp.concatenate(
        [
            lax.ppermute(sea_depth[rows - margin:], "band", down),
            sea_depth,
            lax.ppermute(sea_depth[:margin], "band", up),
        ],
        axis=0,
    )

    height, east_vel, north_vel = state[0], state[1], state[2]
    scattered = jnp.where(jnp.isnan(values), jnp.float32(0.0), values - height)
    spread = smooth(scattered, 1)

    to_below = jnp.concatenate(
        [spread, height[rows - margin:], east_vel[rows - margin:], north_vel[rows - margin:]], axis=0
    )
    to_above = jnp.concatenate(
        [spread, height[:margin], east_vel[:margin], north_vel[:margin]], axis=0
    )
    from_above = lax.ppermute(to_below, "band", down)
    from_below = lax.ppermute(to_above, "band", up)

    total_rows = rows * bands
    ext_rows = rows + 2 * margin
    global_rows = band_start - margin + jnp.arange(ext_rows)
    inside = ((global_rows >= 0) & (global_rows < total_rows)).astype(jnp.float32)[:, None]
    coriolis = (0.1 + 0.4 * ((global_rows.astype(jnp.float32) + 0.5) / total_rows))[:, None]
    wide = (ext_rows, columns)
    out = pl.pallas_call(
        forecast_kernel,
        interpret=INTERPRET,
        out_shape=jax.ShapeDtypeStruct((fields, rows, columns), jnp.float32),
        scratch_shapes=[
            pltpu.VMEM((3 * rows, columns), jnp.float32),
            pltpu.VMEM((ext_rows + 16, columns), jnp.float32),
            pltpu.VMEM(wide, jnp.float32),
            pltpu.VMEM(wide, jnp.float32),
            pltpu.VMEM(wide, jnp.float32),
        ],
    )(
        from_above, from_below, height, east_vel, north_vel, spread, depth_ext,
        jnp.broadcast_to(coriolis, (ext_rows, 128)), jnp.broadcast_to(inside, (ext_rows, 128)),
    )
    return out[None]


def solution(mesh):
    placed = (
        P("dom", None, "band", None),
        P("dom"),
        P("band", None),
        P("band"),
        P("band"),
        P("band"),
    )
    return jax.shard_map(
        on_device,
        mesh=mesh,
        in_specs=placed,
        out_specs=P("dom", None, "band", None),
        check_vma=False,
    )
```

```python
import functools
import numpy as np
import jax
import jax.numpy as jnp
from jax import lax
from jax.sharding import PartitionSpec as P
from jax.experimental import pallas as pl
from jax.experimental.pallas import tpu as pltpu

STEPS = 4
BW = 8


TIME_STEP = 0.8
NUDGE_GAIN = 0.5
LENGTH_SCALE = 3.0
INTERPRET = False


def weights():
    return [np.float32(np.exp(np.float32(-abs(o) / LENGTH_SCALE))) for o in range(-BW, BW + 1)]


def smooth(field, axis_no):
    count = field.shape[axis_no]
    widths = [(0, 0)] * field.ndim
    widths[axis_no] = (BW, BW)
    padded = jnp.pad(field, widths)
    total = jnp.zeros_like(field)
    for offset, weight in zip(range(-BW, BW + 1), weights()):
        piece = lax.slice_in_dim(padded, BW + offset, BW + offset + count, axis=axis_no)
        total = total + weight * piece
    return total


def forecast_kernel(fa_ref, fb_ref, h_ref, u_ref, v_ref, pf_ref, d_ref,
                    o_ref, pad_ref, hx_ref, *, total_rows):
    rows = h_ref.shape[0]
    margin = 2 * STEPS
    ext = rows + 2 * margin
    columns = h_ref.shape[1]
    half = rows // 2
    hx_ref[0:margin] = fa_ref[2 * margin:3 * margin] + NUDGE_GAIN * pf_ref[0:margin]
    hx_ref[margin:margin + half] = h_ref[0:half] + NUDGE_GAIN * (
        pf_ref[margin:margin + half] + fa_ref[margin:2 * margin])
    hx_ref[margin + half:margin + rows] = h_ref[half:rows] + NUDGE_GAIN * (
        pf_ref[margin + half:margin + rows] + fb_ref[margin:2 * margin])
    hx_ref[margin + rows:ext] = fb_ref[2 * margin:3 * margin] + NUDGE_GAIN * pf_ref[margin + rows:ext]
    height = hx_ref[...]
    east_vel = jnp.concatenate([fa_ref[3 * margin:4 * margin], u_ref[...], fb_ref[3 * margin:4 * margin]], axis=0)
    north_vel = jnp.concatenate([fa_ref[0:margin], v_ref[...], fb_ref[0:margin]], axis=0)
    band_start = lax.axis_index("band") * rows
    global_rows = band_start - margin + lax.broadcasted_iota(jnp.int32, (ext, columns), 0)
    inside = (global_rows >= 0) & (global_rows < total_rows)
    coriolis = 0.1 + 0.4 * ((global_rows.astype(jnp.float32) + 0.5) / total_rows)
    depth = d_ref[...]
    pad_ref[0:8] = jnp.zeros((8, columns), jnp.float32)
    pad_ref[8 + ext:16 + ext] = jnp.zeros((8, columns), jnp.float32)

    def north(q):
        pad_ref[8:8 + ext] = q
        return 0.5 * (pad_ref[9:9 + ext] - pad_ref[7:7 + ext])

    def east(q):
        return 0.5 * (pltpu.roll(q, columns - 1, 1) - pltpu.roll(q, 1, 1))

    for _ in range(STEPS):
        flux_east = depth * east_vel
        flux_north = depth * north_vel
        east_diff = east(flux_east)
        north_diff = north(flux_north)
        height = jnp.where(inside, height - TIME_STEP * (east_diff + north_diff), jnp.float32(0.0))
        slope_east = east(height)
        slope_north = north(height)
        new_east = east_vel + TIME_STEP * (coriolis * north_vel - slope_east)
        new_north = north_vel + TIME_STEP * (-coriolis * east_vel - slope_north)
        east_vel, north_vel = new_east, new_north
    o_ref[0] = height[margin:margin + rows]
    o_ref[1] = east_vel[margin:margin + rows]
    o_ref[2] = north_vel[margin:margin + rows]


def on_device(ensemble, ancestors, sea_depth, obs_rows, obs_cols, obs_values):
    _, fields, rows, columns = ensemble.shape
    parts = lax.axis_size("dom")
    bands = lax.axis_size("band")
    band = lax.axis_index("band")
    down = [(i, i + 1) for i in range(bands - 1)]
    up = [(i + 1, i) for i in range(bands - 1)]
    margin = 2 * STEPS

    block = ensemble.reshape(fields * rows, parts, columns // parts).transpose(1, 0, 2)
    tag = jnp.broadcast_to(ancestors.astype(jnp.float32)[:, None, None], (parts, 8, columns // parts))
    crossed = lax.all_to_all(jnp.concatenate([block, tag], axis=1), "dom", 0, 0, tiled=True)
    lineage = crossed[:, fields * rows, 0].astype(jnp.int32)
    chosen = jnp.take(crossed[:, :fields * rows], lineage, axis=0)
    back = lax.all_to_all(chosen, "dom", 0, 0, tiled=True)
    state = back.transpose(1, 0, 2).reshape(fields, rows, columns)

    band_start = band * rows
    position = (obs_rows - band_start) * columns + obs_cols
    values = jnp.full((rows * columns,), jnp.nan, jnp.float32).at[position].set(obs_values)
    values = values.reshape(rows, columns)

    depth_ext = jnp.concatenate(
        [
            lax.ppermute(sea_depth[rows - margin:], "band", down),
            sea_depth,
            lax.ppermute(sea_depth[:margin], "band", up),
        ],
        axis=0,
    )

    height, east_vel, north_vel = state[0], state[1], state[2]
    scattered = jnp.where(jnp.isnan(values), jnp.float32(0.0), values - height)
    spread = smooth(scattered, 1)

    partial = smooth(jnp.pad(spread, ((margin, margin), (0, 0))), 0)
    to_below = jnp.concatenate(
        [
            north_vel[rows - margin:],
            partial[rows + margin:],
            height[rows - margin:] + NUDGE_GAIN * partial[rows:rows + margin],
            east_vel[rows - margin:],
        ],
        axis=0,
    )
    to_above = jnp.concatenate(
        [
            north_vel[:margin],
            partial[:margin],
            height[:margin] + NUDGE_GAIN * partial[margin:2 * margin],
            east_vel[:margin],
        ],
        axis=0,
    )
    from_above = lax.ppermute(to_below, "band", down)
    from_below = lax.ppermute(to_above, "band", up)

    ext_rows = rows + 2 * margin
    out = pl.pallas_call(
        functools.partial(forecast_kernel, total_rows=rows * bands),
        interpret=INTERPRET,
        out_shape=jax.ShapeDtypeStruct((fields, rows, columns), jnp.float32),
        scratch_shapes=[
            pltpu.VMEM((ext_rows + 16, columns), jnp.float32),
            pltpu.VMEM((ext_rows, columns), jnp.float32),
        ],
    )(from_above, from_below, height, east_vel, north_vel, partial, depth_ext)
    return out[None]


def solution(mesh):
    placed = (
        P("dom", None, "band", None),
        P("dom"),
        P("band", None),
        P("band"),
        P("band"),
        P("band"),
    )
    return jax.shard_map(
        on_device,
        mesh=mesh,
        in_specs=placed,
        out_specs=P("dom", None, "band", None),
        check_vma=False,
    )
```

```python
import functools
import numpy as np
import jax
import jax.numpy as jnp
from jax import lax
from jax.sharding import PartitionSpec as P
from jax.experimental import pallas as pl
from jax.experimental.pallas import tpu as pltpu

STEPS = 4
BW = 8


TIME_STEP = 0.8
NUDGE_GAIN = 0.5
LENGTH_SCALE = 3.0
INTERPRET = False


def weights():
    return [np.float32(np.exp(np.float32(-abs(o) / LENGTH_SCALE))) for o in range(-BW, BW + 1)]


def smooth(field, axis_no):
    count = field.shape[axis_no]
    widths = [(0, 0)] * field.ndim
    widths[axis_no] = (BW, BW)
    padded = jnp.pad(field, widths)
    total = jnp.zeros_like(field)
    for offset, weight in zip(range(-BW, BW + 1), weights()):
        piece = lax.slice_in_dim(padded, BW + offset, BW + offset + count, axis=axis_no)
        total = total + weight * piece
    return total


def forecast_kernel(fa_ref, fb_ref, h_ref, u_ref, v_ref, pf_ref, d_ref,
                    o_ref, pad_ref, hx_ref, *, total_rows):
    rows = h_ref.shape[0]
    margin = 2 * STEPS
    ext = rows + 2 * margin
    columns = h_ref.shape[1]
    half = rows // 2
    hx_ref[0:margin] = fa_ref[2 * margin:3 * margin] + NUDGE_GAIN * pf_ref[0:margin]
    hx_ref[margin:margin + half] = h_ref[0:half] + NUDGE_GAIN * (
        pf_ref[margin:margin + half] + fa_ref[margin:2 * margin])
    hx_ref[margin + half:margin + rows] = h_ref[half:rows] + NUDGE_GAIN * (
        pf_ref[margin + half:margin + rows] + fb_ref[margin:2 * margin])
    hx_ref[margin + rows:ext] = fb_ref[2 * margin:3 * margin] + NUDGE_GAIN * pf_ref[margin + rows:ext]
    height = hx_ref[...]
    east_vel = jnp.concatenate([fa_ref[3 * margin:4 * margin], u_ref[...], fb_ref[3 * margin:4 * margin]], axis=0)
    north_vel = jnp.concatenate([fa_ref[0:margin], v_ref[...], fb_ref[0:margin]], axis=0)
    band_start = lax.axis_index("band") * rows
    global_rows = band_start - margin + lax.broadcasted_iota(jnp.int32, (ext, columns), 0)
    inside = (global_rows >= 0) & (global_rows < total_rows)
    coriolis = 0.1 + 0.4 * ((global_rows.astype(jnp.float32) + 0.5) / total_rows)
    depth = d_ref[...]
    pad_ref[0:8] = jnp.zeros((8, columns), jnp.float32)
    pad_ref[8 + ext:16 + ext] = jnp.zeros((8, columns), jnp.float32)

    def north(q):
        pad_ref[8:8 + ext] = q
        return 0.5 * (pad_ref[9:9 + ext] - pad_ref[7:7 + ext])

    def east(q):
        return 0.5 * (pltpu.roll(q, columns - 1, 1) - pltpu.roll(q, 1, 1))

    for _ in range(STEPS):
        flux_east = depth * east_vel
        flux_north = depth * north_vel
        east_diff = east(flux_east)
        north_diff = north(flux_north)
        height = jnp.where(inside, height - TIME_STEP * (east_diff + north_diff), jnp.float32(0.0))
        slope_east = east(height)
        slope_north = north(height)
        new_east = east_vel + TIME_STEP * (coriolis * north_vel - slope_east)
        new_north = north_vel + TIME_STEP * (-coriolis * east_vel - slope_north)
        east_vel, north_vel = new_east, new_north
    o_ref[0] = height[margin:margin + rows]
    o_ref[1] = east_vel[margin:margin + rows]
    o_ref[2] = north_vel[margin:margin + rows]


def prepare_kernel(h_ref, u_ref, v_ref, val_ref, below_ref, above_ref, pf_ref, scr_ref):
    rows, columns = h_ref.shape
    margin = 2 * STEPS
    ext = rows + 2 * margin
    values = val_ref[...]
    height = h_ref[...]
    scattered = jnp.where(values != values, jnp.float32(0.0), values - height)
    column = lax.broadcasted_iota(jnp.int32, (rows, columns), 1)
    spread = jnp.zeros((rows, columns), jnp.float32)
    for offset, weight in zip(range(-BW, BW + 1), weights()):
        if offset == 0:
            piece = scattered
        else:
            piece = pltpu.roll(scattered, (-offset) % columns, 1)
            valid = (column + offset >= 0) & (column + offset < columns)
            piece = jnp.where(valid, piece, jnp.float32(0.0))
        spread = spread + weight * piece
    scr_ref[0:2 * margin] = jnp.zeros((2 * margin, columns), jnp.float32)
    scr_ref[2 * margin:2 * margin + rows] = spread
    scr_ref[2 * margin + rows:4 * margin + rows] = jnp.zeros((2 * margin, columns), jnp.float32)
    partial = jnp.zeros((ext, columns), jnp.float32)
    for offset, weight in zip(range(-BW, BW + 1), weights()):
        lo = margin + offset
        partial = partial + weight * scr_ref[lo:lo + ext]
    pf_ref[...] = partial
    below_ref[0:margin] = v_ref[rows - margin:rows]
    below_ref[margin:2 * margin] = partial[rows + margin:ext]
    below_ref[2 * margin:3 * margin] = h_ref[rows - margin:rows] + NUDGE_GAIN * partial[rows:rows + margin]
    below_ref[3 * margin:4 * margin] = u_ref[rows - margin:rows]
    above_ref[0:margin] = v_ref[0:margin]
    above_ref[margin:2 * margin] = partial[0:margin]
    above_ref[2 * margin:3 * margin] = h_ref[0:margin] + NUDGE_GAIN * partial[margin:2 * margin]
    above_ref[3 * margin:4 * margin] = u_ref[0:margin]


def on_device(ensemble, ancestors, sea_depth, obs_rows, obs_cols, obs_values):
    _, fields, rows, columns = ensemble.shape
    parts = lax.axis_size("dom")
    bands = lax.axis_size("band")
    band = lax.axis_index("band")
    down = [(i, i + 1) for i in range(bands - 1)]
    up = [(i + 1, i) for i in range(bands - 1)]
    margin = 2 * STEPS

    block = ensemble.reshape(fields * rows, parts, columns // parts).transpose(1, 0, 2)
    tag = jnp.broadcast_to(ancestors.astype(jnp.float32)[:, None, None], (parts, 8, columns // parts))
    crossed = lax.all_to_all(jnp.concatenate([block, tag], axis=1), "dom", 0, 0, tiled=True)
    lineage = crossed[:, fields * rows, 0].astype(jnp.int32)
    chosen = jnp.take(crossed[:, :fields * rows], lineage, axis=0, mode="clip")
    back = lax.all_to_all(chosen, "dom", 0, 0, tiled=True)
    state = back.transpose(1, 0, 2).reshape(fields, rows, columns)

    band_start = band * rows
    position = (obs_rows - band_start) * columns + obs_cols
    values = jnp.full((rows * columns,), jnp.nan, jnp.float32).at[position].set(obs_values)
    values = values.reshape(rows, columns)

    depth_ext = jnp.concatenate(
        [
            lax.ppermute(sea_depth[rows - margin:], "band", down),
            sea_depth,
            lax.ppermute(sea_depth[:margin], "band", up),
        ],
        axis=0,
    )

    height, east_vel, north_vel = state[0], state[1], state[2]
    halo = jax.ShapeDtypeStruct((4 * margin, columns), jnp.float32)
    to_below, to_above, partial = pl.pallas_call(
        prepare_kernel,
        interpret=INTERPRET,
        out_shape=(halo, halo, jax.ShapeDtypeStruct((rows + 2 * margin, columns), jnp.float32)),
        scratch_shapes=[pltpu.VMEM((rows + 4 * margin, columns), jnp.float32)],
    )(height, east_vel, north_vel, values)
    from_above = lax.ppermute(to_below, "band", down)
    from_below = lax.ppermute(to_above, "band", up)

    ext_rows = rows + 2 * margin
    out = pl.pallas_call(
        functools.partial(forecast_kernel, total_rows=rows * bands),
        interpret=INTERPRET,
        out_shape=jax.ShapeDtypeStruct((fields, rows, columns), jnp.float32),
        scratch_shapes=[
            pltpu.VMEM((ext_rows + 16, columns), jnp.float32),
            pltpu.VMEM((ext_rows, columns), jnp.float32),
        ],
    )(from_above, from_below, height, east_vel, north_vel, partial, depth_ext)
    return out[None]


def solution(mesh):
    placed = (
        P("dom", None, "band", None),
        P("dom"),
        P("band", None),
        P("band"),
        P("band"),
        P("band"),
    )
    return jax.shard_map(
        on_device,
        mesh=mesh,
        in_specs=placed,
        out_specs=P("dom", None, "band", None),
        check_vma=False,
    )
```

```python
import functools
import numpy as np
import jax
import jax.numpy as jnp
from jax import lax
from jax.sharding import PartitionSpec as P
from jax.experimental import pallas as pl
from jax.experimental.pallas import tpu as pltpu

STEPS = 4
BW = 8


TIME_STEP = 0.8
NUDGE_GAIN = 0.5
LENGTH_SCALE = 3.0
INTERPRET = False


def weights():
    return [np.float32(np.exp(np.float32(-abs(o) / LENGTH_SCALE))) for o in range(-BW, BW + 1)]


def smooth(field, axis_no):
    count = field.shape[axis_no]
    widths = [(0, 0)] * field.ndim
    widths[axis_no] = (BW, BW)
    padded = jnp.pad(field, widths)
    total = jnp.zeros_like(field)
    for offset, weight in zip(range(-BW, BW + 1), weights()):
        piece = lax.slice_in_dim(padded, BW + offset, BW + offset + count, axis=axis_no)
        total = total + weight * piece
    return total


def forecast_kernel(fa_ref, fb_ref, h_ref, u_ref, v_ref, pf_ref, d_ref,
                    o_ref, pad_ref, hx_ref, *, total_rows):
    rows = h_ref.shape[0]
    margin = 2 * STEPS
    ext = rows + 2 * margin
    columns = h_ref.shape[1]
    half = rows // 2
    hx_ref[0:margin] = fa_ref[2 * margin:3 * margin] + NUDGE_GAIN * pf_ref[0:margin]
    hx_ref[margin:margin + half] = h_ref[0:half] + NUDGE_GAIN * (
        pf_ref[margin:margin + half] + fa_ref[margin:2 * margin])
    hx_ref[margin + half:margin + rows] = h_ref[half:rows] + NUDGE_GAIN * (
        pf_ref[margin + half:margin + rows] + fb_ref[margin:2 * margin])
    hx_ref[margin + rows:ext] = fb_ref[2 * margin:3 * margin] + NUDGE_GAIN * pf_ref[margin + rows:ext]
    height = hx_ref[...]
    east_vel = jnp.concatenate([fa_ref[3 * margin:4 * margin], u_ref[...], fb_ref[3 * margin:4 * margin]], axis=0)
    north_vel = jnp.concatenate([fa_ref[0:margin], v_ref[...], fb_ref[0:margin]], axis=0)
    band_start = lax.axis_index("band") * rows
    global_rows = band_start - margin + lax.broadcasted_iota(jnp.int32, (ext, columns), 0)
    inside = (global_rows >= 0) & (global_rows < total_rows)
    coriolis = 0.1 + 0.4 * ((global_rows.astype(jnp.float32) + 0.5) / total_rows)
    depth = d_ref[...]
    pad_ref[0:8] = jnp.zeros((8, columns), jnp.float32)
    pad_ref[8 + ext:16 + ext] = jnp.zeros((8, columns), jnp.float32)

    def north(q):
        pad_ref[8:8 + ext] = q
        return 0.5 * (pad_ref[9:9 + ext] - pad_ref[7:7 + ext])

    def east(q):
        return 0.5 * (pltpu.roll(q, columns - 1, 1) - pltpu.roll(q, 1, 1))

    for _ in range(STEPS):
        flux_east = depth * east_vel
        flux_north = depth * north_vel
        east_diff = east(flux_east)
        north_diff = north(flux_north)
        height = jnp.where(inside, height - TIME_STEP * (east_diff + north_diff), jnp.float32(0.0))
        slope_east = east(height)
        slope_north = north(height)
        new_east = east_vel + TIME_STEP * (coriolis * north_vel - slope_east)
        new_north = north_vel + TIME_STEP * (-coriolis * east_vel - slope_north)
        east_vel, north_vel = new_east, new_north
    o_ref[0] = height[margin:margin + rows]
    o_ref[1] = east_vel[margin:margin + rows]
    o_ref[2] = north_vel[margin:margin + rows]


def on_device(ensemble, ancestors, sea_depth, obs_rows, obs_cols, obs_values):
    _, fields, rows, columns = ensemble.shape
    parts = lax.axis_size("dom")
    bands = lax.axis_size("band")
    band = lax.axis_index("band")
    down = [(i, i + 1) for i in range(bands - 1)]
    up = [(i + 1, i) for i in range(bands - 1)]
    margin = 2 * STEPS

    block = ensemble.reshape(fields * rows, parts, columns // parts).transpose(1, 0, 2)
    tag = jnp.broadcast_to(ancestors.astype(jnp.float32)[:, None, None], (parts, 8, columns // parts))
    crossed = lax.all_to_all(jnp.concatenate([block, tag], axis=1), "dom", 0, 0, tiled=True)
    lineage = crossed[:, fields * rows, 0].astype(jnp.int32)
    chosen = jnp.take(crossed[:, :fields * rows], lineage, axis=0, mode="clip")
    back = lax.all_to_all(chosen, "dom", 0, 0, tiled=True)
    state = back.transpose(1, 0, 2).reshape(fields, rows, columns)

    band_start = band * rows
    position = (obs_rows - band_start) * columns + obs_cols
    values = jnp.full((rows * columns,), jnp.nan, jnp.float32).at[position].set(obs_values)
    values = values.reshape(rows, columns)

    depth_ext = jnp.concatenate(
        [
            lax.ppermute(sea_depth[rows - margin:], "band", down),
            sea_depth,
            lax.ppermute(sea_depth[:margin], "band", up),
        ],
        axis=0,
    )

    height, east_vel, north_vel = state[0], state[1], state[2]
    scattered = jnp.where(jnp.isnan(values), jnp.float32(0.0), values - height)
    spread = smooth(scattered, 1)

    partial = smooth(jnp.pad(spread, ((margin, margin), (0, 0))), 0)
    to_below = jnp.concatenate(
        [
            north_vel[rows - margin:],
            partial[rows + margin:],
            height[rows - margin:] + NUDGE_GAIN * partial[rows:rows + margin],
            east_vel[rows - margin:],
        ],
        axis=0,
    )
    to_above = jnp.concatenate(
        [
            north_vel[:margin],
            partial[:margin],
            height[:margin] + NUDGE_GAIN * partial[margin:2 * margin],
            east_vel[:margin],
        ],
        axis=0,
    )
    from_above = lax.ppermute(to_below, "band", down)
    from_below = lax.ppermute(to_above, "band", up)

    ext_rows = rows + 2 * margin
    out = pl.pallas_call(
        functools.partial(forecast_kernel, total_rows=rows * bands),
        interpret=INTERPRET,
        out_shape=jax.ShapeDtypeStruct((fields, rows, columns), jnp.float32),
        scratch_shapes=[
            pltpu.VMEM((ext_rows + 16, columns), jnp.float32),
            pltpu.VMEM((ext_rows, columns), jnp.float32),
        ],
    )(from_above, from_below, height, east_vel, north_vel, partial, depth_ext)
    return out[None]


def solution(mesh):
    placed = (
        P("dom", None, "band", None),
        P("dom"),
        P("band", None),
        P("band"),
        P("band"),
        P("band"),
    )
    return jax.shard_map(
        on_device,
        mesh=mesh,
        in_specs=placed,
        out_specs=P("dom", None, "band", None),
        check_vma=False,
    )
```

```python
import functools
import numpy as np
import jax
import jax.numpy as jnp
from jax import lax
from jax.sharding import PartitionSpec as P
from jax.experimental import pallas as pl
from jax.experimental.pallas import tpu as pltpu

STEPS = 4
BW = 8


TIME_STEP = 0.8
NUDGE_GAIN = 0.5
LENGTH_SCALE = 3.0
INTERPRET = False


def weights():
    return [np.float32(np.exp(np.float32(-abs(o) / LENGTH_SCALE))) for o in range(-BW, BW + 1)]


def smooth(field, axis_no):
    count = field.shape[axis_no]
    widths = [(0, 0)] * field.ndim
    widths[axis_no] = (BW, BW)
    padded = jnp.pad(field, widths)
    total = jnp.zeros_like(field)
    for offset, weight in zip(range(-BW, BW + 1), weights()):
        piece = lax.slice_in_dim(padded, BW + offset, BW + offset + count, axis=axis_no)
        total = total + weight * piece
    return total


def forecast_kernel(fa_ref, fb_ref, h_ref, u_ref, v_ref, pf_ref, d_ref,
                    o_ref, pad_ref, hx_ref, *, total_rows):
    rows = h_ref.shape[0]
    margin = 2 * STEPS
    ext = rows + 2 * margin
    columns = h_ref.shape[1]
    half = rows // 2
    hx_ref[0:margin] = fa_ref[2 * margin:3 * margin] + NUDGE_GAIN * pf_ref[0:margin]
    hx_ref[margin:margin + half] = h_ref[0:half] + NUDGE_GAIN * (
        pf_ref[margin:margin + half] + fa_ref[margin:2 * margin])
    hx_ref[margin + half:margin + rows] = h_ref[half:rows] + NUDGE_GAIN * (
        pf_ref[margin + half:margin + rows] + fb_ref[margin:2 * margin])
    hx_ref[margin + rows:ext] = fb_ref[2 * margin:3 * margin] + NUDGE_GAIN * pf_ref[margin + rows:ext]
    height = hx_ref[...]
    east_vel = jnp.concatenate([fa_ref[3 * margin:4 * margin], u_ref[...], fb_ref[3 * margin:4 * margin]], axis=0)
    north_vel = jnp.concatenate([fa_ref[0:margin], v_ref[...], fb_ref[0:margin]], axis=0)
    band_start = lax.axis_index("band") * rows
    global_rows = band_start - margin + lax.broadcasted_iota(jnp.int32, (ext, columns), 0)
    inside = (global_rows >= 0) & (global_rows < total_rows)
    coriolis = 0.1 + 0.4 * ((global_rows.astype(jnp.float32) + 0.5) / total_rows)
    depth = d_ref[...]
    pad_ref[0:8] = jnp.zeros((8, columns), jnp.float32)
    pad_ref[8 + ext:16 + ext] = jnp.zeros((8, columns), jnp.float32)

    def north(q):
        pad_ref[8:8 + ext] = q
        return 0.5 * (pad_ref[9:9 + ext] - pad_ref[7:7 + ext])

    def east(q):
        return 0.5 * (pltpu.roll(q, columns - 1, 1) - pltpu.roll(q, 1, 1))

    for _ in range(STEPS):
        flux_east = depth * east_vel
        flux_north = depth * north_vel
        east_diff = east(flux_east)
        north_diff = north(flux_north)
        height = jnp.where(inside, height - TIME_STEP * (east_diff + north_diff), jnp.float32(0.0))
        slope_east = east(height)
        slope_north = north(height)
        new_east = east_vel + TIME_STEP * (coriolis * north_vel - slope_east)
        new_north = north_vel + TIME_STEP * (-coriolis * east_vel - slope_north)
        east_vel, north_vel = new_east, new_north
    o_ref[0] = height[margin:margin + rows]
    o_ref[1] = east_vel[margin:margin + rows]
    o_ref[2] = north_vel[margin:margin + rows]


def on_device(ensemble, ancestors, sea_depth, obs_rows, obs_cols, obs_values):
    _, fields, rows, columns = ensemble.shape
    parts = lax.axis_size("dom")
    bands = lax.axis_size("band")
    band = lax.axis_index("band")
    down = [(i, i + 1) for i in range(bands - 1)]
    up = [(i + 1, i) for i in range(bands - 1)]
    margin = 2 * STEPS

    block = ensemble.reshape(fields * rows, parts, columns // parts).transpose(1, 0, 2)
    tag = jnp.broadcast_to(ancestors.astype(jnp.float32)[:, None, None], (parts, 8, columns // parts))
    crossed = lax.all_to_all(jnp.concatenate([block, tag], axis=1), "dom", 0, 0, tiled=True)
    lineage = crossed[:, fields * rows, 0].astype(jnp.int32)
    chosen = jnp.take(crossed[:, :fields * rows], lineage, axis=0, mode="clip")
    back = lax.all_to_all(chosen, "dom", 0, 0, tiled=True)
    state = back.transpose(1, 0, 2).reshape(fields, rows, columns)

    band_start = band * rows
    position = (obs_rows - band_start) * columns + obs_cols
    values = jnp.full((rows * columns,), jnp.nan, jnp.float32).at[position].set(obs_values)
    values = values.reshape(rows, columns)

    depth_ext = jnp.concatenate(
        [
            lax.ppermute(sea_depth[rows - margin:], "band", down),
            sea_depth,
            lax.ppermute(sea_depth[:margin], "band", up),
        ],
        axis=0,
    )

    height, east_vel, north_vel = state[0], state[1], state[2]
    scattered = jnp.where(jnp.isnan(values), jnp.float32(0.0), values - height)
    spread = smooth(scattered, 1)

    partial = smooth(jnp.pad(spread, ((margin, margin), (0, 0))), 0)
    to_below = jnp.concatenate(
        [
            north_vel[rows - margin:],
            partial[rows + margin:],
            height[rows - margin:] + NUDGE_GAIN * partial[rows:rows + margin],
            east_vel[rows - margin:],
        ],
        axis=0,
    )
    to_above = jnp.concatenate(
        [
            north_vel[:margin],
            partial[:margin],
            height[:margin] + NUDGE_GAIN * partial[margin:2 * margin],
            east_vel[:margin],
        ],
        axis=0,
    )
    ring_down = [(i, (i + 1) % bands) for i in range(bands)]
    ring_up = [((i + 1) % bands, i) for i in range(bands)]
    from_above = jnp.where(band > 0, lax.ppermute(to_below, "band", ring_down), jnp.float32(0.0))
    from_below = jnp.where(band < bands - 1, lax.ppermute(to_above, "band", ring_up), jnp.float32(0.0))

    ext_rows = rows + 2 * margin
    out = pl.pallas_call(
        functools.partial(forecast_kernel, total_rows=rows * bands),
        interpret=INTERPRET,
        out_shape=jax.ShapeDtypeStruct((fields, rows, columns), jnp.float32),
        scratch_shapes=[
            pltpu.VMEM((ext_rows + 16, columns), jnp.float32),
            pltpu.VMEM((ext_rows, columns), jnp.float32),
        ],
    )(from_above, from_below, height, east_vel, north_vel, partial, depth_ext)
    return out[None]


def solution(mesh):
    placed = (
        P("dom", None, "band", None),
        P("dom"),
        P("band", None),
        P("band"),
        P("band"),
        P("band"),
    )
    return jax.shard_map(
        on_device,
        mesh=mesh,
        in_specs=placed,
        out_specs=P("dom", None, "band", None),
        check_vma=False,
    )
```

```python
import functools
import numpy as np
import jax
import jax.numpy as jnp
from jax import lax
from jax.sharding import PartitionSpec as P
from jax.experimental import pallas as pl
from jax.experimental.pallas import tpu as pltpu

STEPS = 4
BW = 8


TIME_STEP = 0.8
NUDGE_GAIN = 0.5
LENGTH_SCALE = 3.0
INTERPRET = False


def weights():
    return [np.float32(np.exp(np.float32(-abs(o) / LENGTH_SCALE))) for o in range(-BW, BW + 1)]


def smooth(field, axis_no):
    count = field.shape[axis_no]
    widths = [(0, 0)] * field.ndim
    widths[axis_no] = (BW, BW)
    padded = jnp.pad(field, widths)
    total = jnp.zeros_like(field)
    for offset, weight in zip(range(-BW, BW + 1), weights()):
        piece = lax.slice_in_dim(padded, BW + offset, BW + offset + count, axis=axis_no)
        total = total + weight * piece
    return total


def forecast_kernel(fa_ref, fb_ref, h_ref, u_ref, v_ref, pf_ref, d_ref,
                    o_ref, pad_ref, hx_ref, *, total_rows):
    rows = h_ref.shape[0]
    margin = 2 * STEPS
    ext = rows + 2 * margin
    columns = h_ref.shape[1]
    half = rows // 2
    band = lax.axis_index("band")
    keep_above = jnp.where(band > 0, jnp.float32(1.0), jnp.float32(0.0))
    keep_below = jnp.where(band < total_rows // rows - 1, jnp.float32(1.0), jnp.float32(0.0))

    def above(lo, hi):
        return fa_ref[lo:hi] * keep_above

    def below(lo, hi):
        return fb_ref[lo:hi] * keep_below

    hx_ref[0:margin] = above(2 * margin, 3 * margin) + NUDGE_GAIN * pf_ref[0:margin]
    hx_ref[margin:margin + half] = h_ref[0:half] + NUDGE_GAIN * (
        pf_ref[margin:margin + half] + above(margin, 2 * margin))
    hx_ref[margin + half:margin + rows] = h_ref[half:rows] + NUDGE_GAIN * (
        pf_ref[margin + half:margin + rows] + below(margin, 2 * margin))
    hx_ref[margin + rows:ext] = below(2 * margin, 3 * margin) + NUDGE_GAIN * pf_ref[margin + rows:ext]
    height = hx_ref[...]
    east_vel = jnp.concatenate([above(3 * margin, 4 * margin), u_ref[...], below(3 * margin, 4 * margin)], axis=0)
    north_vel = jnp.concatenate([above(0, margin), v_ref[...], below(0, margin)], axis=0)
    band_start = band * rows
    global_rows = band_start - margin + lax.broadcasted_iota(jnp.int32, (ext, columns), 0)
    inside = (global_rows >= 0) & (global_rows < total_rows)
    coriolis = 0.1 + 0.4 * ((global_rows.astype(jnp.float32) + 0.5) / total_rows)
    depth = d_ref[...]
    pad_ref[0:8] = jnp.zeros((8, columns), jnp.float32)
    pad_ref[8 + ext:16 + ext] = jnp.zeros((8, columns), jnp.float32)

    def north(q):
        pad_ref[8:8 + ext] = q
        return 0.5 * (pad_ref[9:9 + ext] - pad_ref[7:7 + ext])

    def east(q):
        return 0.5 * (pltpu.roll(q, columns - 1, 1) - pltpu.roll(q, 1, 1))

    for _ in range(STEPS):
        flux_east = depth * east_vel
        flux_north = depth * north_vel
        east_diff = east(flux_east)
        north_diff = north(flux_north)
        height = jnp.where(inside, height - TIME_STEP * (east_diff + north_diff), jnp.float32(0.0))
        slope_east = east(height)
        slope_north = north(height)
        new_east = east_vel + TIME_STEP * (coriolis * north_vel - slope_east)
        new_north = north_vel + TIME_STEP * (-coriolis * east_vel - slope_north)
        east_vel, north_vel = new_east, new_north
    o_ref[0] = height[margin:margin + rows]
    o_ref[1] = east_vel[margin:margin + rows]
    o_ref[2] = north_vel[margin:margin + rows]


def on_device(ensemble, ancestors, sea_depth, obs_rows, obs_cols, obs_values):
    _, fields, rows, columns = ensemble.shape
    parts = lax.axis_size("dom")
    bands = lax.axis_size("band")
    band = lax.axis_index("band")
    down = [(i, i + 1) for i in range(bands - 1)]
    up = [(i + 1, i) for i in range(bands - 1)]
    margin = 2 * STEPS

    block = ensemble.reshape(fields * rows, parts, columns // parts).transpose(1, 0, 2)
    tag = jnp.broadcast_to(ancestors.astype(jnp.float32)[:, None, None], (parts, 8, columns // parts))
    crossed = lax.all_to_all(jnp.concatenate([block, tag], axis=1), "dom", 0, 0, tiled=True)
    lineage = crossed[:, fields * rows, 0].astype(jnp.int32)
    chosen = jnp.take(crossed[:, :fields * rows], lineage, axis=0, mode="clip")
    back = lax.all_to_all(chosen, "dom", 0, 0, tiled=True)
    state = back.transpose(1, 0, 2).reshape(fields, rows, columns)

    band_start = band * rows
    position = (obs_rows - band_start) * columns + obs_cols
    values = jnp.full((rows * columns,), jnp.nan, jnp.float32).at[position].set(obs_values)
    values = values.reshape(rows, columns)

    depth_ext = jnp.concatenate(
        [
            lax.ppermute(sea_depth[rows - margin:], "band", down),
            sea_depth,
            lax.ppermute(sea_depth[:margin], "band", up),
        ],
        axis=0,
    )

    height, east_vel, north_vel = state[0], state[1], state[2]
    scattered = jnp.where(jnp.isnan(values), jnp.float32(0.0), values - height)
    spread = smooth(scattered, 1)

    partial = smooth(jnp.pad(spread, ((margin, margin), (0, 0))), 0)
    to_below = jnp.concatenate(
        [
            north_vel[rows - margin:],
            partial[rows + margin:],
            height[rows - margin:] + NUDGE_GAIN * partial[rows:rows + margin],
            east_vel[rows - margin:],
        ],
        axis=0,
    )
    to_above = jnp.concatenate(
        [
            north_vel[:margin],
            partial[:margin],
            height[:margin] + NUDGE_GAIN * partial[margin:2 * margin],
            east_vel[:margin],
        ],
        axis=0,
    )
    ring_down = [(i, (i + 1) % bands) for i in range(bands)]
    ring_up = [((i + 1) % bands, i) for i in range(bands)]
    from_above = lax.ppermute(to_below, "band", ring_down)
    from_below = lax.ppermute(to_above, "band", ring_up)

    ext_rows = rows + 2 * margin
    out = pl.pallas_call(
        functools.partial(forecast_kernel, total_rows=rows * bands),
        interpret=INTERPRET,
        out_shape=jax.ShapeDtypeStruct((fields, rows, columns), jnp.float32),
        scratch_shapes=[
            pltpu.VMEM((ext_rows + 16, columns), jnp.float32),
            pltpu.VMEM((ext_rows, columns), jnp.float32),
        ],
    )(from_above, from_below, height, east_vel, north_vel, partial, depth_ext)
    return out[None]


def solution(mesh):
    placed = (
        P("dom", None, "band", None),
        P("dom"),
        P("band", None),
        P("band"),
        P("band"),
        P("band"),
    )
    return jax.shard_map(
        on_device,
        mesh=mesh,
        in_specs=placed,
        out_specs=P("dom", None, "band", None),
        check_vma=False,
    )
```

```python
import functools
import numpy as np
import jax
import jax.numpy as jnp
from jax import lax
from jax.sharding import PartitionSpec as P
from jax.experimental import pallas as pl
from jax.experimental.pallas import tpu as pltpu

STEPS = 4
BW = 8


TIME_STEP = 0.8
NUDGE_GAIN = 0.5
LENGTH_SCALE = 3.0
INTERPRET = False


def weights():
    return [np.float32(np.exp(np.float32(-abs(o) / LENGTH_SCALE))) for o in range(-BW, BW + 1)]


def smooth(field, axis_no):
    count = field.shape[axis_no]
    widths = [(0, 0)] * field.ndim
    widths[axis_no] = (BW, BW)
    padded = jnp.pad(field, widths)
    total = jnp.zeros_like(field)
    for offset, weight in zip(range(-BW, BW + 1), weights()):
        piece = lax.slice_in_dim(padded, BW + offset, BW + offset + count, axis=axis_no)
        total = total + weight * piece
    return total


def forecast_kernel(fa_ref, fb_ref, h_ref, u_ref, v_ref, pf_ref, d_ref,
                    o_ref, pad_ref, hx_ref, *, total_rows):
    rows = h_ref.shape[0]
    margin = 2 * STEPS
    ext = rows + 2 * margin
    columns = h_ref.shape[1]
    half = rows // 2
    band = lax.axis_index("band")
    keep_above = jnp.where(band > 0, jnp.float32(1.0), jnp.float32(0.0))
    keep_below = jnp.where(band < total_rows // rows - 1, jnp.float32(1.0), jnp.float32(0.0))

    def above(lo, hi):
        return fa_ref[lo:hi] * keep_above

    def below(lo, hi):
        return fb_ref[lo:hi] * keep_below

    hx_ref[0:margin] = above(2 * margin, 3 * margin) + NUDGE_GAIN * pf_ref[0:margin]
    hx_ref[margin:margin + half] = h_ref[0:half] + NUDGE_GAIN * (
        pf_ref[margin:margin + half] + above(margin, 2 * margin))
    hx_ref[margin + half:margin + rows] = h_ref[half:rows] + NUDGE_GAIN * (
        pf_ref[margin + half:margin + rows] + below(margin, 2 * margin))
    hx_ref[margin + rows:ext] = below(2 * margin, 3 * margin) + NUDGE_GAIN * pf_ref[margin + rows:ext]
    height = hx_ref[...]
    east_vel = jnp.concatenate([above(3 * margin, 4 * margin), u_ref[...], below(3 * margin, 4 * margin)], axis=0)
    north_vel = jnp.concatenate([above(0, margin), v_ref[...], below(0, margin)], axis=0)
    band_start = band * rows
    global_rows = band_start - margin + lax.broadcasted_iota(jnp.int32, (ext, columns), 0)
    inside = (global_rows >= 0) & (global_rows < total_rows)
    coriolis = 0.1 + 0.4 * ((global_rows.astype(jnp.float32) + 0.5) / total_rows)
    depth = d_ref[...]
    pad_ref[0:8] = jnp.zeros((8, columns), jnp.float32)
    pad_ref[8 + ext:16 + ext] = jnp.zeros((8, columns), jnp.float32)

    def north(q):
        pad_ref[8:8 + ext] = q
        return 0.5 * (pad_ref[9:9 + ext] - pad_ref[7:7 + ext])

    def east(q):
        return 0.5 * (pltpu.roll(q, columns - 1, 1) - pltpu.roll(q, 1, 1))

    for _ in range(STEPS):
        flux_east = depth * east_vel
        flux_north = depth * north_vel
        east_diff = east(flux_east)
        north_diff = north(flux_north)
        height = jnp.where(inside, height - TIME_STEP * (east_diff + north_diff), jnp.float32(0.0))
        slope_east = east(height)
        slope_north = north(height)
        new_east = east_vel + TIME_STEP * (coriolis * north_vel - slope_east)
        new_north = north_vel + TIME_STEP * (-coriolis * east_vel - slope_north)
        east_vel, north_vel = new_east, new_north
    o_ref[0] = height[margin:margin + rows]
    o_ref[1] = east_vel[margin:margin + rows]
    o_ref[2] = north_vel[margin:margin + rows]


def on_device(ensemble, ancestors, sea_depth, obs_rows, obs_cols, obs_values):
    _, fields, rows, columns = ensemble.shape
    parts = lax.axis_size("dom")
    bands = lax.axis_size("band")
    band = lax.axis_index("band")
    down = [(i, i + 1) for i in range(bands - 1)]
    up = [(i + 1, i) for i in range(bands - 1)]
    margin = 2 * STEPS

    block = ensemble.reshape(fields * rows, parts, columns // parts).transpose(1, 0, 2)
    tag = jnp.broadcast_to(ancestors.astype(jnp.float32)[:, None, None], (parts, 8, columns // parts))
    crossed = lax.all_to_all(jnp.concatenate([block, tag], axis=1), "dom", 0, 0, tiled=True)
    lineage = crossed[:, fields * rows, 0].astype(jnp.int32)
    chosen = jnp.take(crossed[:, :fields * rows], lineage, axis=0, mode="clip")
    back = lax.all_to_all(chosen, "dom", 0, 0, tiled=True)
    state = back.transpose(1, 0, 2).reshape(fields, rows, columns)

    band_start = band * rows
    position = (obs_rows - band_start) * columns + obs_cols
    values = jnp.full((rows * columns,), jnp.nan, jnp.float32).at[position].set(obs_values)
    values = values.reshape(rows, columns)

    depth_ext = jnp.concatenate(
        [
            lax.ppermute(sea_depth[rows - margin:], "band", down),
            sea_depth,
            lax.ppermute(sea_depth[:margin], "band", up),
        ],
        axis=0,
    )

    height, east_vel, north_vel = state[0], state[1], state[2]
    scattered = jnp.where(jnp.isnan(values), jnp.float32(0.0), values - height)
    spread = smooth(scattered, 1)

    partial = smooth(jnp.pad(spread, ((margin, margin), (0, 0))), 0)
    to_below = jnp.concatenate(
        [
            north_vel[rows - margin:],
            partial[rows + margin:],
            height[rows - margin:] + NUDGE_GAIN * partial[rows:rows + margin],
            east_vel[rows - margin:],
        ],
        axis=0,
    )
    to_above = jnp.concatenate(
        [
            north_vel[:margin],
            partial[:margin],
            height[:margin] + NUDGE_GAIN * partial[margin:2 * margin],
            east_vel[:margin],
        ],
        axis=0,
    )
    ring_down = [(i, (i + 1) % bands) for i in range(bands)]
    ring_up = [((i + 1) % bands, i) for i in range(bands)]
    from_above = lax.ppermute(to_below, "band", ring_down)
    from_below = lax.ppermute(to_above, "band", ring_up)

    ext_rows = rows + 2 * margin
    out = pl.pallas_call(
        functools.partial(forecast_kernel, total_rows=rows * bands),
        interpret=INTERPRET,
        out_shape=jax.ShapeDtypeStruct((fields, rows, columns), jnp.float32),
        in_specs=[pl.BlockSpec(memory_space=pltpu.VMEM)] * 7,
        scratch_shapes=[
            pltpu.VMEM((ext_rows + 16, columns), jnp.float32),
            pltpu.VMEM((ext_rows, columns), jnp.float32),
        ],
    )(*[pltpu.with_memory_space_constraint(x, pltpu.VMEM)
        for x in (from_above, from_below, height, east_vel, north_vel, partial, depth_ext)])
    return out[None]


def solution(mesh):
    placed = (
        P("dom", None, "band", None),
        P("dom"),
        P("band", None),
        P("band"),
        P("band"),
        P("band"),
    )
    return jax.shard_map(
        on_device,
        mesh=mesh,
        in_specs=placed,
        out_specs=P("dom", None, "band", None),
        check_vma=False,
    )
```

```python
import functools
import numpy as np
import jax
import jax.numpy as jnp
from jax import lax
from jax.sharding import PartitionSpec as P
from jax.experimental import pallas as pl
from jax.experimental.pallas import tpu as pltpu

STEPS = 4
BW = 8


TIME_STEP = 0.8
NUDGE_GAIN = 0.5
LENGTH_SCALE = 3.0
INTERPRET = False


def weights():
    return [np.float32(np.exp(np.float32(-abs(o) / LENGTH_SCALE))) for o in range(-BW, BW + 1)]


def smooth(field, axis_no):
    count = field.shape[axis_no]
    widths = [(0, 0)] * field.ndim
    widths[axis_no] = (BW, BW)
    padded = jnp.pad(field, widths)
    total = jnp.zeros_like(field)
    for offset, weight in zip(range(-BW, BW + 1), weights()):
        piece = lax.slice_in_dim(padded, BW + offset, BW + offset + count, axis=axis_no)
        total = total + weight * piece
    return total


def forecast_kernel(fa_ref, fb_ref, h_ref, u_ref, v_ref, pf_ref, d_ref,
                    o_ref, pad_ref, hx_ref, *, total_rows):
    rows = h_ref.shape[0]
    margin = 2 * STEPS
    ext = rows + 2 * margin
    columns = h_ref.shape[1]
    half = rows // 2
    band = lax.axis_index("band")
    keep_above = jnp.where(band > 0, jnp.float32(1.0), jnp.float32(0.0))
    keep_below = jnp.where(band < total_rows // rows - 1, jnp.float32(1.0), jnp.float32(0.0))

    def above(lo, hi):
        return fa_ref[lo:hi] * keep_above

    def below(lo, hi):
        return fb_ref[lo:hi] * keep_below

    hx_ref[0:margin] = above(2 * margin, 3 * margin) + NUDGE_GAIN * pf_ref[0:margin]
    hx_ref[margin:margin + half] = h_ref[0:half] + NUDGE_GAIN * (
        pf_ref[margin:margin + half] + above(margin, 2 * margin))
    hx_ref[margin + half:margin + rows] = h_ref[half:rows] + NUDGE_GAIN * (
        pf_ref[margin + half:margin + rows] + below(margin, 2 * margin))
    hx_ref[margin + rows:ext] = below(2 * margin, 3 * margin) + NUDGE_GAIN * pf_ref[margin + rows:ext]
    height = hx_ref[...]
    east_vel = jnp.concatenate([above(3 * margin, 4 * margin), u_ref[...], below(3 * margin, 4 * margin)], axis=0)
    north_vel = jnp.concatenate([above(0, margin), v_ref[...], below(0, margin)], axis=0)
    band_start = band * rows
    global_rows = band_start - margin + lax.broadcasted_iota(jnp.int32, (ext, columns), 0)
    inside = (global_rows >= 0) & (global_rows < total_rows)
    coriolis = 0.1 + 0.4 * ((global_rows.astype(jnp.float32) + 0.5) / total_rows)
    depth = d_ref[...]
    pad_ref[0:8] = jnp.zeros((8, columns), jnp.float32)
    pad_ref[8 + ext:16 + ext] = jnp.zeros((8, columns), jnp.float32)

    def north(q):
        pad_ref[8:8 + ext] = q
        return 0.5 * (pad_ref[9:9 + ext] - pad_ref[7:7 + ext])

    def east(q):
        return 0.5 * (pltpu.roll(q, columns - 1, 1) - pltpu.roll(q, 1, 1))

    for _ in range(STEPS):
        flux_east = depth * east_vel
        flux_north = depth * north_vel
        east_diff = east(flux_east)
        north_diff = north(flux_north)
        height = jnp.where(inside, height - TIME_STEP * (east_diff + north_diff), jnp.float32(0.0))
        slope_east = east(height)
        slope_north = north(height)
        new_east = east_vel + TIME_STEP * (coriolis * north_vel - slope_east)
        new_north = north_vel + TIME_STEP * (-coriolis * east_vel - slope_north)
        east_vel, north_vel = new_east, new_north
    o_ref[0] = height[margin:margin + rows]
    o_ref[1] = east_vel[margin:margin + rows]
    o_ref[2] = north_vel[margin:margin + rows]


def take_kernel(lineage_ref, src_ref, out_ref, sems):
    count, rows = out_ref.shape[0], out_ref.shape[1]
    copies = []
    for c in range(count):
        copy = pltpu.make_async_copy(src_ref.at[lineage_ref[c], pl.ds(0, rows)], out_ref.at[c], sems.at[c])
        copy.start()
        copies.append(copy)
    for copy in copies:
        copy.wait()


def on_device(ensemble, ancestors, sea_depth, obs_rows, obs_cols, obs_values):
    _, fields, rows, columns = ensemble.shape
    parts = lax.axis_size("dom")
    bands = lax.axis_size("band")
    band = lax.axis_index("band")
    down = [(i, i + 1) for i in range(bands - 1)]
    up = [(i + 1, i) for i in range(bands - 1)]
    margin = 2 * STEPS

    block = ensemble.reshape(fields * rows, parts, columns // parts).transpose(1, 0, 2)
    tag = jnp.broadcast_to(ancestors.astype(jnp.float32)[:, None, None], (parts, 8, columns // parts))
    crossed = lax.all_to_all(jnp.concatenate([block, tag], axis=1), "dom", 0, 0, tiled=True)
    lineage = jnp.clip(crossed[:, fields * rows, 0].astype(jnp.int32), 0, parts - 1)
    chosen = pl.pallas_call(
        take_kernel,
        interpret=INTERPRET,
        out_shape=jax.ShapeDtypeStruct((parts, fields * rows, columns // parts), jnp.float32),
        grid_spec=pltpu.PrefetchScalarGridSpec(
            num_scalar_prefetch=1,
            grid=(1,),
            in_specs=[pl.BlockSpec(memory_space=pl.ANY)],
            out_specs=pl.BlockSpec(memory_space=pl.ANY),
            scratch_shapes=[pltpu.SemaphoreType.DMA((parts,))],
        ),
    )(lineage, pltpu.with_memory_space_constraint(crossed, pltpu.VMEM))
    back = lax.all_to_all(chosen, "dom", 0, 0, tiled=True)
    state = back.transpose(1, 0, 2).reshape(fields, rows, columns)

    band_start = band * rows
    position = (obs_rows - band_start) * columns + obs_cols
    values = jnp.full((rows * columns,), jnp.nan, jnp.float32).at[position].set(obs_values)
    values = values.reshape(rows, columns)

    depth_ext = jnp.concatenate(
        [
            lax.ppermute(sea_depth[rows - margin:], "band", down),
            sea_depth,
            lax.ppermute(sea_depth[:margin], "band", up),
        ],
        axis=0,
    )

    height, east_vel, north_vel = state[0], state[1], state[2]
    scattered = jnp.where(jnp.isnan(values), jnp.float32(0.0), values - height)
    spread = smooth(scattered, 1)

    partial = smooth(jnp.pad(spread, ((margin, margin), (0, 0))), 0)
    to_below = jnp.concatenate(
        [
            north_vel[rows - margin:],
            partial[rows + margin:],
            height[rows - margin:] + NUDGE_GAIN * partial[rows:rows + margin],
            east_vel[rows - margin:],
        ],
        axis=0,
    )
    to_above = jnp.concatenate(
        [
            north_vel[:margin],
            partial[:margin],
            height[:margin] + NUDGE_GAIN * partial[margin:2 * margin],
            east_vel[:margin],
        ],
        axis=0,
    )
    ring_down = [(i, (i + 1) % bands) for i in range(bands)]
    ring_up = [((i + 1) % bands, i) for i in range(bands)]
    from_above = lax.ppermute(to_below, "band", ring_down)
    from_below = lax.ppermute(to_above, "band", ring_up)

    ext_rows = rows + 2 * margin
    out = pl.pallas_call(
        functools.partial(forecast_kernel, total_rows=rows * bands),
        interpret=INTERPRET,
        out_shape=jax.ShapeDtypeStruct((fields, rows, columns), jnp.float32),
        in_specs=[pl.BlockSpec(memory_space=pltpu.VMEM)] * 7,
        scratch_shapes=[
            pltpu.VMEM((ext_rows + 16, columns), jnp.float32),
            pltpu.VMEM((ext_rows, columns), jnp.float32),
        ],
    )(*[pltpu.with_memory_space_constraint(x, pltpu.VMEM)
        for x in (from_above, from_below, height, east_vel, north_vel, partial, depth_ext)])
    return out[None]


def solution(mesh):
    placed = (
        P("dom", None, "band", None),
        P("dom"),
        P("band", None),
        P("band"),
        P("band"),
        P("band"),
    )
    return jax.shard_map(
        on_device,
        mesh=mesh,
        in_specs=placed,
        out_specs=P("dom", None, "band", None),
        check_vma=False,
    )
```

```python
import functools
import numpy as np
import jax
import jax.numpy as jnp
from jax import lax
from jax.sharding import PartitionSpec as P
from jax.experimental import pallas as pl
from jax.experimental.pallas import tpu as pltpu

STEPS = 4
BW = 8


TIME_STEP = 0.8
NUDGE_GAIN = 0.5
LENGTH_SCALE = 3.0
INTERPRET = False


def weights():
    return [np.float32(np.exp(np.float32(-abs(o) / LENGTH_SCALE))) for o in range(-BW, BW + 1)]


def smooth(field, axis_no):
    count = field.shape[axis_no]
    widths = [(0, 0)] * field.ndim
    widths[axis_no] = (BW, BW)
    padded = jnp.pad(field, widths)
    total = jnp.zeros_like(field)
    for offset, weight in zip(range(-BW, BW + 1), weights()):
        piece = lax.slice_in_dim(padded, BW + offset, BW + offset + count, axis=axis_no)
        total = total + weight * piece
    return total


def forecast_kernel(fa_ref, fb_ref, h_ref, u_ref, v_ref, pf_ref, d_ref,
                    o_ref, pad_ref, hx_ref, *, total_rows):
    rows = h_ref.shape[0]
    margin = 2 * STEPS
    ext = rows + 2 * margin
    columns = h_ref.shape[1]
    half = rows // 2
    band = lax.axis_index("band")
    keep_above = jnp.where(band > 0, jnp.float32(1.0), jnp.float32(0.0))
    keep_below = jnp.where(band < total_rows // rows - 1, jnp.float32(1.0), jnp.float32(0.0))

    def above(lo, hi):
        return fa_ref[lo:hi] * keep_above

    def below(lo, hi):
        return fb_ref[lo:hi] * keep_below

    hx_ref[0:margin] = above(2 * margin, 3 * margin) + NUDGE_GAIN * pf_ref[0:margin]
    hx_ref[margin:margin + half] = h_ref[0:half] + NUDGE_GAIN * (
        pf_ref[margin:margin + half] + above(margin, 2 * margin))
    hx_ref[margin + half:margin + rows] = h_ref[half:rows] + NUDGE_GAIN * (
        pf_ref[margin + half:margin + rows] + below(margin, 2 * margin))
    hx_ref[margin + rows:ext] = below(2 * margin, 3 * margin) + NUDGE_GAIN * pf_ref[margin + rows:ext]
    height = hx_ref[...]
    east_vel = jnp.concatenate([above(3 * margin, 4 * margin), u_ref[...], below(3 * margin, 4 * margin)], axis=0)
    north_vel = jnp.concatenate([above(0, margin), v_ref[...], below(0, margin)], axis=0)
    band_start = band * rows
    global_rows = band_start - margin + lax.broadcasted_iota(jnp.int32, (ext, columns), 0)
    inside = (global_rows >= 0) & (global_rows < total_rows)
    coriolis = 0.1 + 0.4 * ((global_rows.astype(jnp.float32) + 0.5) / total_rows)
    depth = d_ref[...]
    pad_ref[0:8] = jnp.zeros((8, columns), jnp.float32)
    pad_ref[8 + ext:16 + ext] = jnp.zeros((8, columns), jnp.float32)

    def north(q):
        pad_ref[8:8 + ext] = q
        return 0.5 * (pad_ref[9:9 + ext] - pad_ref[7:7 + ext])

    def east(q):
        return 0.5 * (pltpu.roll(q, columns - 1, 1) - pltpu.roll(q, 1, 1))

    for _ in range(STEPS):
        flux_east = depth * east_vel
        flux_north = depth * north_vel
        east_diff = east(flux_east)
        north_diff = north(flux_north)
        height = jnp.where(inside, height - TIME_STEP * (east_diff + north_diff), jnp.float32(0.0))
        slope_east = east(height)
        slope_north = north(height)
        new_east = east_vel + TIME_STEP * (coriolis * north_vel - slope_east)
        new_north = north_vel + TIME_STEP * (-coriolis * east_vel - slope_north)
        east_vel, north_vel = new_east, new_north
    o_ref[0] = height[margin:margin + rows]
    o_ref[1] = east_vel[margin:margin + rows]
    o_ref[2] = north_vel[margin:margin + rows]


def on_device(ensemble, ancestors, sea_depth, obs_rows, obs_cols, obs_values):
    _, fields, rows, columns = ensemble.shape
    parts = lax.axis_size("dom")
    bands = lax.axis_size("band")
    band = lax.axis_index("band")
    down = [(i, i + 1) for i in range(bands - 1)]
    up = [(i + 1, i) for i in range(bands - 1)]
    margin = 2 * STEPS

    block = ensemble.reshape(fields * rows, parts, columns // parts).transpose(1, 0, 2)
    tag = jnp.broadcast_to(ancestors.astype(jnp.float32)[:, None, None], (parts, 8, columns // parts))
    crossed = lax.all_to_all(jnp.concatenate([block, tag], axis=1), "dom", 0, 0, tiled=True)
    lineage = crossed[:, fields * rows, 0].astype(jnp.int32)
    chosen = jnp.take(crossed[:, :fields * rows], lineage, axis=0, mode="clip")
    back = lax.all_to_all(chosen, "dom", 0, 0, tiled=True)
    state = back.transpose(1, 0, 2).reshape(fields, rows, columns)

    band_start = band * rows
    position = (obs_rows - band_start) * columns + obs_cols
    values = jnp.full((rows * columns,), jnp.nan, jnp.float32).at[position].set(obs_values)
    values = values.reshape(rows, columns)

    depth_ext = jnp.concatenate(
        [
            lax.ppermute(sea_depth[rows - margin:], "band", down),
            sea_depth,
            lax.ppermute(sea_depth[:margin], "band", up),
        ],
        axis=0,
    )

    height, east_vel, north_vel = state[0], state[1], state[2]
    scattered = jnp.where(jnp.isnan(values), jnp.float32(0.0), values - height)
    spread = smooth(scattered, 1)

    partial = smooth(jnp.pad(spread, ((margin, margin), (0, 0))), 0)
    to_below = jnp.concatenate(
        [
            north_vel[rows - margin:],
            partial[rows + margin:],
            height[rows - margin:] + NUDGE_GAIN * partial[rows:rows + margin],
            east_vel[rows - margin:],
        ],
        axis=0,
    )
    to_above = jnp.concatenate(
        [
            north_vel[:margin],
            partial[:margin],
            height[:margin] + NUDGE_GAIN * partial[margin:2 * margin],
            east_vel[:margin],
        ],
        axis=0,
    )
    ring_up = [((i + 1) % bands, i) for i in range(bands)]
    from_above = lax.ppermute(to_below, "band", down)
    from_below = lax.ppermute(to_above, "band", ring_up)

    ext_rows = rows + 2 * margin
    out = pl.pallas_call(
        functools.partial(forecast_kernel, total_rows=rows * bands),
        interpret=INTERPRET,
        out_shape=jax.ShapeDtypeStruct((fields, rows, columns), jnp.float32),
        in_specs=[pl.BlockSpec(memory_space=pltpu.VMEM)] * 7,
        scratch_shapes=[
            pltpu.VMEM((ext_rows + 16, columns), jnp.float32),
            pltpu.VMEM((ext_rows, columns), jnp.float32),
        ],
    )(*[pltpu.with_memory_space_constraint(x, pltpu.VMEM)
        for x in (from_above, from_below, height, east_vel, north_vel, partial, depth_ext)])
    return out[None]


def solution(mesh):
    placed = (
        P("dom", None, "band", None),
        P("dom"),
        P("band", None),
        P("band"),
        P("band"),
        P("band"),
    )
    return jax.shard_map(
        on_device,
        mesh=mesh,
        in_specs=placed,
        out_specs=P("dom", None, "band", None),
        check_vma=False,
    )
```

```python
import functools
import numpy as np
import jax
import jax.numpy as jnp
from jax import lax
from jax.sharding import PartitionSpec as P
from jax.experimental import pallas as pl
from jax.experimental.pallas import tpu as pltpu

STEPS = 4
BW = 8


TIME_STEP = 0.8
NUDGE_GAIN = 0.5
LENGTH_SCALE = 3.0
INTERPRET = False


def weights():
    return [np.float32(np.exp(np.float32(-abs(o) / LENGTH_SCALE))) for o in range(-BW, BW + 1)]


def smooth(field, axis_no):
    count = field.shape[axis_no]
    widths = [(0, 0)] * field.ndim
    widths[axis_no] = (BW, BW)
    padded = jnp.pad(field, widths)
    total = jnp.zeros_like(field)
    for offset, weight in zip(range(-BW, BW + 1), weights()):
        piece = lax.slice_in_dim(padded, BW + offset, BW + offset + count, axis=axis_no)
        total = total + weight * piece
    return total


def forecast_kernel(fa_ref, fb_ref, h_ref, u_ref, v_ref, pf_ref, d_ref,
                    o_ref, pad_ref, hx_ref, *, total_rows):
    rows = h_ref.shape[0]
    margin = 2 * STEPS
    ext = rows + 2 * margin
    columns = h_ref.shape[1]
    half = rows // 2
    band = lax.axis_index("band")
    keep_below = jnp.where(band < total_rows // rows - 1, jnp.float32(1.0), jnp.float32(0.0))

    def above(lo, hi):
        return fa_ref[lo:hi]

    def below(lo, hi):
        return fb_ref[lo:hi] * keep_below

    hx_ref[0:margin] = above(2 * margin, 3 * margin) + NUDGE_GAIN * pf_ref[0:margin]
    hx_ref[margin:margin + half] = h_ref[0:half] + NUDGE_GAIN * (
        pf_ref[margin:margin + half] + above(margin, 2 * margin))
    hx_ref[margin + half:margin + rows] = h_ref[half:rows] + NUDGE_GAIN * (
        pf_ref[margin + half:margin + rows] + below(margin, 2 * margin))
    hx_ref[margin + rows:ext] = below(2 * margin, 3 * margin) + NUDGE_GAIN * pf_ref[margin + rows:ext]
    height = hx_ref[...]
    east_vel = jnp.concatenate([above(3 * margin, 4 * margin), u_ref[...], below(3 * margin, 4 * margin)], axis=0)
    north_vel = jnp.concatenate([above(0, margin), v_ref[...], below(0, margin)], axis=0)
    band_start = band * rows
    global_rows = band_start - margin + lax.broadcasted_iota(jnp.int32, (ext, 1), 0)
    inside = jnp.broadcast_to((global_rows >= 0) & (global_rows < total_rows), (ext, columns))
    coriolis = jnp.broadcast_to(0.1 + 0.4 * ((global_rows.astype(jnp.float32) + 0.5) / total_rows), (ext, columns))
    depth = d_ref[...]
    pad_ref[0:8] = jnp.zeros((8, columns), jnp.float32)
    pad_ref[8 + ext:16 + ext] = jnp.zeros((8, columns), jnp.float32)

    def north(q):
        pad_ref[8:8 + ext] = q
        return 0.5 * (pad_ref[9:9 + ext] - pad_ref[7:7 + ext])

    def east(q):
        return 0.5 * (pltpu.roll(q, columns - 1, 1) - pltpu.roll(q, 1, 1))

    for _ in range(STEPS):
        flux_east = depth * east_vel
        flux_north = depth * north_vel
        east_diff = east(flux_east)
        north_diff = north(flux_north)
        height = jnp.where(inside, height - TIME_STEP * (east_diff + north_diff), jnp.float32(0.0))
        slope_east = east(height)
        slope_north = north(height)
        new_east = east_vel + TIME_STEP * (coriolis * north_vel - slope_east)
        new_north = north_vel + TIME_STEP * (-coriolis * east_vel - slope_north)
        east_vel, north_vel = new_east, new_north
    o_ref[0] = height[margin:margin + rows]
    o_ref[1] = east_vel[margin:margin + rows]
    o_ref[2] = north_vel[margin:margin + rows]


def on_device(ensemble, ancestors, sea_depth, obs_rows, obs_cols, obs_values):
    _, fields, rows, columns = ensemble.shape
    parts = lax.axis_size("dom")
    bands = lax.axis_size("band")
    band = lax.axis_index("band")
    down = [(i, i + 1) for i in range(bands - 1)]
    up = [(i + 1, i) for i in range(bands - 1)]
    margin = 2 * STEPS

    block = ensemble.reshape(fields * rows, parts, columns // parts).transpose(1, 0, 2)
    tag = jnp.broadcast_to(ancestors.astype(jnp.float32)[:, None, None], (parts, 8, columns // parts))
    crossed = lax.all_to_all(jnp.concatenate([block, tag], axis=1), "dom", 0, 0, tiled=True)
    lineage = crossed[:, fields * rows, 0].astype(jnp.int32)
    chosen = jnp.take(crossed[:, :fields * rows], lineage, axis=0, mode="clip")
    back = lax.all_to_all(chosen, "dom", 0, 0, tiled=True)
    state = back.transpose(1, 0, 2).reshape(fields, rows, columns)

    band_start = band * rows
    position = (obs_rows - band_start) * columns + obs_cols
    values = jnp.full((rows * columns,), jnp.nan, jnp.float32).at[position].set(obs_values)
    values = values.reshape(rows, columns)

    depth_ext = jnp.concatenate(
        [
            lax.ppermute(sea_depth[rows - margin:], "band", down),
            sea_depth,
            lax.ppermute(sea_depth[:margin], "band", up),
        ],
        axis=0,
    )

    height, east_vel, north_vel = state[0], state[1], state[2]
    scattered = jnp.where(jnp.isnan(values), jnp.float32(0.0), values - height)
    spread = smooth(scattered, 1)

    partial = smooth(jnp.pad(spread, ((margin, margin), (0, 0))), 0)
    to_below = jnp.concatenate(
        [
            north_vel[rows - margin:],
            partial[rows + margin:],
            height[rows - margin:] + NUDGE_GAIN * partial[rows:rows + margin],
            east_vel[rows - margin:],
        ],
        axis=0,
    )
    to_above = jnp.concatenate(
        [
            north_vel[:margin],
            partial[:margin],
            height[:margin] + NUDGE_GAIN * partial[margin:2 * margin],
            east_vel[:margin],
        ],
        axis=0,
    )
    ring_up = [((i + 1) % bands, i) for i in range(bands)]
    from_above = lax.ppermute(to_below, "band", down)
    from_below = lax.ppermute(to_above, "band", ring_up)

    ext_rows = rows + 2 * margin
    out = pl.pallas_call(
        functools.partial(forecast_kernel, total_rows=rows * bands),
        interpret=INTERPRET,
        out_shape=jax.ShapeDtypeStruct((fields, rows, columns), jnp.float32),
        in_specs=[pl.BlockSpec(memory_space=pltpu.VMEM)] * 7,
        scratch_shapes=[
            pltpu.VMEM((ext_rows + 16, columns), jnp.float32),
            pltpu.VMEM((ext_rows, columns), jnp.float32),
        ],
    )(*[pltpu.with_memory_space_constraint(x, pltpu.VMEM)
        for x in (from_above, from_below, height, east_vel, north_vel, partial, depth_ext)])
    return out[None]


def solution(mesh):
    placed = (
        P("dom", None, "band", None),
        P("dom"),
        P("band", None),
        P("band"),
        P("band"),
        P("band"),
    )

    return jax.shard_map(
        on_device,
        mesh=mesh,
        in_specs=placed,
        out_specs=P("dom", None, "band", None),
        check_vma=False,
    )
```
